32 devices in a mesh: groups: 2 (over x), seq: 8 (over z, y), samp: 2 (over core).
Axes of the slice: x: 2, y: 2, z: 4, core: 2. Of those that a mesh axis runs over, the one named last changes fastest.
Arguments:
- q_proj: bfloat16 [4, 2048, 4096], P(('groups', 'samp'), 'seq'), parts along dimension 0, may hold values from -750 to 750
- q_tangent: bfloat16 [4, 2048, 4096], P(('groups', 'samp'), 'seq'), parts along dimension 0, may hold values from -750 to 750
- k_proj: bfloat16 [4, 2048, 4096], P(('groups', 'samp'), 'seq'), parts along dimension 0, may hold values from -750 to 750
- k_tangent: bfloat16 [4, 2048, 4096], P(('groups', 'samp'), 'seq'), parts along dimension 0, may hold values from -750 to 750
- v_proj: bfloat16 [4, 2048, 4096], P(('groups', 'samp'), 'seq'), parts along dimension 0, may hold values from -6 to 6
- v_tangent: bfloat16 [4, 2048, 4096], P(('groups', 'samp'), 'seq'), parts along dimension 0, may hold values from -6 to 6
- query_norm_gain: float32 [4096], replicated, may hold values from 0.5 to 2
- key_norm_gain: float32 [4096], replicated, may hold values from 0.5 to 2
- lengths: int32 [4, 4], P('groups'), parts along dimension 0, may hold values from 1 to 768, 2048 in all within a row
Outputs:
- attended: float32 [4, 2048, 4096], P(('groups', 'samp'), 'seq'), parts along dimension 0
- attended_tangent: float32 [4, 2048, 4096], P(('groups', 'samp'), 'seq'), parts along dimension 0
The draws below stay inside these ranges and needn't reach their ends.
There are 2 independent parts, one for each index of `groups`. The reference program is written for one: setup_inputs(seed, part) draws one part's arguments, and reference() takes and returns one part's arrays. A program takes and returns all parts, laid end to end along the dimension named above; an argument that names none is the same for every part. Nothing has to cross between parts.
Inputs may be any that keep to these rules, and one draw needn't show every extreme that they name: `lengths`: each row sums to 2048 and its largest entry is 768.
All inputs are finite; a program needn't handle non-finite values.
Results may differ from the reference program's by a relative error of at most 0.022.
The reference program's roundings to bfloat16 on the way count: a program that leaves them out, or rounds other values in their place, can miss the bound.
Values may be sent and summed in bfloat16 or wider, within the bound.
No kernel may reach another device: no remote copies, remote signals or barrier semaphores. Data moves between devices by JAX's collectives and lax.ppermute only.
A program may use at most 128 MiB of HBM per device.

```python
import math
import jax
import jax.numpy as jnp
import numpy as np
from jax import lax

HEADS = 32
HEAD_DIM = 128
SAMPLES = 4
D = 4096
PACK = 2048
PACKS = 2
MOST = 768


def base_field(key, tag):
    row_key, column_key, noise_key = jax.random.split(jax.random.fold_in(key, tag), 3)
    row_scale = jnp.exp(jax.random.uniform(row_key, (PACKS, PACK, 1), jnp.float32, 0.0, math.log(10.0)))
    column_scale = jnp.exp(jax.random.uniform(column_key, (1, 1, D), jnp.float32, 0.0, math.log(10.0)))
    noise = jnp.clip(jax.random.normal(noise_key, (PACKS, PACK, D), jnp.float32), -5.0, 5.0)
    return noise * row_scale * column_scale


def query_field(key):
    field = base_field(key, 1)
    return field


def key_field(key):
    field = base_field(key, 3)
    return field


def draw_q_proj(key, part):
    return query_field(key).astype(jnp.bfloat16)


def draw_q_tangent(key, part):
    return (0.5 * query_field(key) + base_field(key, 2)).astype(jnp.bfloat16)


def draw_k_proj(key, part):
    return key_field(key).astype(jnp.bfloat16)


def draw_k_tangent(key, part):
    return (0.5 * key_field(key) + base_field(key, 4)).astype(jnp.bfloat16)


def level_of(key, shape, pieces, smallest, largest):
    def one(axis_at, blocks):
        heights = jax.random.uniform(jax.random.fold_in(jax.random.fold_in(key, 6), axis_at), (blocks,), jnp.float32, smallest / len(pieces), largest / len(pieces))
        return jnp.repeat(jnp.exp(heights), shape[axis_at] // blocks).reshape((-1,) + (1,) * (len(shape) - axis_at - 1))

    loudness = one(*pieces[0])
    for cut in pieces[1:]:
        loudness = loudness * one(*cut)
    return loudness


def profile(amount, total, most, slope):
    loads = [(1 << 20) // math.isqrt(grade ** slope) + 1 for grade in range(2, amount + 1)]
    rest, counts = total - most - (amount - 1), [1] * (amount - 1)
    while rest > 0:
        candidates = [i for i in range(amount - 1) if counts[i] < most]
        mass, remaining = sum([loads[i] for i in candidates]), rest
        for i in candidates:
            addition = min(most - counts[i], max(1, remaining * loads[i] // mass), rest)
            counts[i] = counts[i] + addition
            rest = rest - addition
    return np.array([most] + counts)


def uneven_parts(stream_key, number_of, total, bound, slope):
    if number_of == 2:
        one = jax.random.randint(stream_key, (), max(1, total - bound), min(bound, total - 1) + 1)
        return jnp.stack([one, total - one])
    sizes = jnp.asarray(profile(number_of, total, bound, slope), jnp.int32)
    twos = (number_of - 1) // 2
    giver, receiver = sizes[1:1 + 2 * twos:2], sizes[2:2 + 2 * twos:2]
    margin = jnp.minimum(giver - 1, bound - receiver)
    shifted = jax.random.randint(jax.random.fold_in(stream_key, 1), (twos,), 0, 1 << 20) % (margin + 1)
    sizes = sizes.at[1:1 + 2 * twos:2].set(giver - shifted).at[2:2 + 2 * twos:2].set(receiver + shifted)
    return sizes[jax.random.permutation(jax.random.fold_in(stream_key, 2), number_of)]


def normal_values(key, extent, deviation, bound, cuts=(), kind=jnp.bfloat16):
    drawn = jax.random.normal(key, extent, jnp.float32) * deviation
    if len(cuts) > 0:
        drawn = level_of(key, extent, cuts, -0.22, 0.18) * drawn
    return jnp.clip(drawn, min=-bound, max=bound).astype(kind)


def setup_inputs(seed: int = 0, part: int = 0) -> dict:
    key_list = jax.random.split(jax.random.key(seed), 10)
    part_keys = jax.random.split(jax.random.fold_in(key_list[9], part), 10)
    q_proj = draw_q_proj(jax.random.fold_in(jax.random.fold_in(key_list[9], part), 71), part)
    q_tangent = draw_q_tangent(jax.random.fold_in(jax.random.fold_in(key_list[9], part), 71), part)
    k_proj = draw_k_proj(jax.random.fold_in(jax.random.fold_in(key_list[9], part), 71), part)
    k_tangent = draw_k_tangent(jax.random.fold_in(jax.random.fold_in(key_list[9], part), 71), part)
    v_proj = normal_values(part_keys[4], (PACKS, PACK, D), 1.0, 6.0, ((0, 2), (1, 8)))
    v_tangent = normal_values(part_keys[5], (PACKS, PACK, D), 1.0, 6.0, ((0, 2), (1, 8)))
    query_norm_gain = jnp.clip(jnp.exp(jax.random.uniform(key_list[6], (D,), jnp.float32, math.log(0.5), math.log(2.0))), 0.5, 2.0)
    key_norm_gain = jnp.clip(jnp.exp(jax.random.uniform(key_list[7], (D,), jnp.float32, math.log(0.5), math.log(2.0))), 0.5, 2.0)
    lengths = jax.vmap(lambda own: uneven_parts(own, SAMPLES, PACK, MOST, 2))(jax.random.split(part_keys[8], PACKS)).reshape((PACKS, SAMPLES)).astype(jnp.int32)
    return dict(q_proj=q_proj, q_tangent=q_tangent, k_proj=k_proj, k_tangent=k_tangent, v_proj=v_proj, v_tangent=v_tangent, query_norm_gain=query_norm_gain, key_norm_gain=key_norm_gain, lengths=lengths)


def normalize(source, source_tangent, gain):
    widened = source.astype(jnp.float32)
    dwidened = source_tangent.astype(jnp.float32)
    inverse = lax.rsqrt(lax.optimization_barrier(jnp.mean(widened * widened, axis=-1, keepdims=True)) + 1e-06)
    radial = lax.optimization_barrier(jnp.mean(widened * dwidened, axis=-1, keepdims=True))
    normed = (widened * inverse * gain).astype(jnp.bfloat16)
    tangent = ((dwidened * inverse - widened * inverse ** 3 * radial) * gain).astype(jnp.bfloat16)
    return (normed, tangent)

def segment_ids(sample_lengths):
    sample_ends = jnp.cumsum(sample_lengths).astype(jnp.int32)
    positions = jnp.arange(PACK, dtype=jnp.int32)
    return lax.optimization_barrier(jnp.sum((positions[:, None] >= sample_ends[None, :]).astype(jnp.int32), axis=1)).astype(jnp.int32)

def one_head(operands, same_sample):
    queries, keys, values, dqueries, dkeys, dvalues = operands
    factor = 1.0 / math.sqrt(HEAD_DIM)
    logit_scores = jnp.dot(queries, keys.T, preferred_element_type=jnp.float32) * factor
    logit_scores = jnp.where(same_sample, logit_scores, -1e+30)
    row_top = lax.optimization_barrier(jnp.max(logit_scores, axis=1, keepdims=True))
    exponent = jnp.exp(logit_scores - row_top)
    weights = exponent / lax.optimization_barrier(jnp.sum(exponent, axis=1, keepdims=True))
    dscores = (jnp.dot(dqueries, keys.T, preferred_element_type=jnp.float32) + jnp.dot(queries, dkeys.T, preferred_element_type=jnp.float32)) * factor
    dscores = jnp.where(same_sample, dscores, 0.0)
    center = lax.optimization_barrier(jnp.sum(weights * dscores, axis=1, keepdims=True))
    rounded = weights.astype(jnp.bfloat16)
    spread = (weights * dscores).astype(jnp.bfloat16)
    output = jnp.dot(rounded, values, preferred_element_type=jnp.float32)
    tangent = jnp.dot(spread, values, preferred_element_type=jnp.float32) - center * output + jnp.dot(rounded, dvalues, preferred_element_type=jnp.float32)
    return (output, tangent)

def reference(q_proj, q_tangent, k_proj, k_tangent, v_proj, v_tangent, query_norm_gain, key_norm_gain, lengths):
    q_normed, dq_normed = normalize(q_proj, q_tangent, query_norm_gain)
    k_normed, dk_normed = normalize(k_proj, k_tangent, key_norm_gain)
    outputs = []
    tangents = []
    for pack_index in range(PACKS):
        segment = segment_ids(lengths[pack_index])
        same_sample = segment[:, None] == segment[None, :]
        arrays = tuple((jnp.transpose(array[pack_index].reshape(PACK, HEADS, HEAD_DIM), (1, 0, 2)) for array in (q_normed, k_normed, v_proj, dq_normed, dk_normed, v_tangent)))
        output, tangent = lax.map(lambda operands: one_head(operands, same_sample), arrays)
        outputs.append(jnp.transpose(output, (1, 0, 2)).reshape(PACK, D))
        tangents.append(jnp.transpose(tangent, (1, 0, 2)).reshape(PACK, D))
    return (jnp.stack(outputs), jnp.stack(tangents))
```

```python
import functools
import math

import jax
import jax.numpy as jnp
from jax import lax
from jax.experimental import pallas as pl
from jax.experimental.pallas import tpu as pltpu
from jax.sharding import PartitionSpec as P

HEAD_DIM = 128
BLOCK = 256


def normalize(source, source_tangent, gain):
    widened = source.astype(jnp.float32)
    dwidened = source_tangent.astype(jnp.float32)
    inverse = lax.rsqrt(jnp.mean(widened * widened, axis=-1, keepdims=True) + 1e-06)
    radial = jnp.mean(widened * dwidened, axis=-1, keepdims=True)
    normed = (widened * inverse * gain).astype(jnp.bfloat16)
    tangent = ((dwidened * inverse - widened * inverse**3 * radial) * gain).astype(jnp.bfloat16)
    return (normed, tangent)


def block_tables(sample_lengths, count):
    sample_ends = jnp.cumsum(sample_lengths).astype(jnp.int32)
    sample_starts = sample_ends - sample_lengths
    blocks = count // BLOCK
    first_rows = jnp.arange(blocks, dtype=jnp.int32) * BLOCK
    last_rows = first_rows + (BLOCK - 1)
    first_segment = jnp.sum((first_rows[:, None] >= sample_ends[None, :]).astype(jnp.int32), axis=1)
    last_segment = jnp.sum((last_rows[:, None] >= sample_ends[None, :]).astype(jnp.int32), axis=1)
    samples = sample_lengths.shape[0]
    first_segment = jnp.clip(first_segment, 0, samples - 1)
    last_segment = jnp.clip(last_segment, 0, samples - 1)
    first_key = jnp.take(sample_starts, first_segment)
    last_key = jnp.take(sample_ends, last_segment)
    first_block = jnp.clip(first_key // BLOCK, 0, blocks - 1)
    last_block = jnp.clip((last_key - 1) // BLOCK + 1, first_block + 1, blocks)
    return first_block.astype(jnp.int32), last_block.astype(jnp.int32), sample_ends


def attention_kernel(
    first_ref, last_ref, ends_ref,
    q_ref, dq_ref, k_ref, dk_ref, v_ref, dv_ref,
    out_ref, tan_ref,
):
    i = pl.program_id(1)
    samples = ends_ref.shape[0]
    factor = 1.0 / math.sqrt(HEAD_DIM)
    queries = q_ref[...]
    dqueries = dq_ref[...]
    both_queries = jnp.concatenate([dqueries, queries], axis=1)

    def segment_of(positions):
        seg = jnp.zeros(positions.shape, jnp.int32)
        for j in range(samples):
            seg = seg + (positions >= ends_ref[j]).astype(jnp.int32)
        return seg

    query_positions = i * BLOCK + lax.broadcasted_iota(jnp.int32, (BLOCK, 1), 0)
    query_segment = segment_of(query_positions)
    first = first_ref[i]
    last = last_ref[i]

    def scores_of(kb):
        start = pl.multiple_of(kb * BLOCK, BLOCK)
        key_rows = k_ref[pl.ds(start, BLOCK), :]
        key_positions = start + lax.broadcasted_iota(jnp.int32, (1, BLOCK), 1)
        same = query_segment == segment_of(key_positions)
        raw = lax.dot_general(
            queries, key_rows, (((1,), (1,)), ((), ())), preferred_element_type=jnp.float32
        ) * factor
        return raw, same, start, key_rows

    def statistics(kb, carry):
        row_top, total = carry
        raw, same, _, _ = scores_of(kb)
        masked = jnp.where(same, raw, -1e30)
        new_top = jnp.maximum(row_top, jnp.max(masked, axis=1, keepdims=True))
        exponent = jnp.where(same, jnp.exp(masked - new_top), 0.0)
        total = total * jnp.exp(row_top - new_top) + jnp.sum(exponent, axis=1, keepdims=True)
        return new_top, total

    row_top, total = lax.fori_loop(
        first, last, statistics,
        (jnp.full((BLOCK, 1), -1e30, jnp.float32), jnp.zeros((BLOCK, 1), jnp.float32)),
    )
    inverse_total = 1.0 / total

    def sums(kb, carry):
        center, output, spread_sum, dvalue_sum = carry
        raw, same, start, key_rows = scores_of(kb)
        dkey_rows = dk_ref[pl.ds(start, BLOCK), :]
        value_rows = v_ref[pl.ds(start, BLOCK), :]
        dvalue_rows = dv_ref[pl.ds(start, BLOCK), :]
        both_keys = jnp.concatenate([key_rows, dkey_rows], axis=1)
        dscores = lax.dot_general(
            both_queries, both_keys, (((1,), (1,)), ((), ())), preferred_element_type=jnp.float32
        ) * factor
        weights = jnp.where(same, jnp.exp(raw - row_top), 0.0) * inverse_total
        product = jnp.where(same, weights * dscores, 0.0)
        center = center + jnp.sum(product, axis=1, keepdims=True)
        rounded = weights.astype(jnp.bfloat16)
        spread = product.astype(jnp.bfloat16)
        output = output + jnp.dot(rounded, value_rows, preferred_element_type=jnp.float32)
        spread_sum = spread_sum + jnp.dot(spread, value_rows, preferred_element_type=jnp.float32)
        dvalue_sum = dvalue_sum + jnp.dot(rounded, dvalue_rows, preferred_element_type=jnp.float32)
        return center, output, spread_sum, dvalue_sum

    empty = jnp.zeros((BLOCK, HEAD_DIM), jnp.float32)
    center, output, spread_sum, dvalue_sum = lax.fori_loop(
        first, last, sums, (jnp.zeros((BLOCK, 1), jnp.float32), empty, empty, empty)
    )
    out_ref[...] = output
    tan_ref[...] = spread_sum - center * output + dvalue_sum


def attend(q, dq, k, dk, v, dv, first_block, last_block, sample_ends):
    tokens, width = q.shape
    heads = width // HEAD_DIM
    blocks = tokens // BLOCK
    query_spec = pl.BlockSpec((BLOCK, HEAD_DIM), lambda h, i, *_: (i, h))
    key_spec = pl.BlockSpec((tokens, HEAD_DIM), lambda h, i, *_: (0, h))
    grid_spec = pltpu.PrefetchScalarGridSpec(
        num_scalar_prefetch=3,
        grid=(heads, blocks),
        in_specs=[query_spec, query_spec, key_spec, key_spec, key_spec, key_spec],
        out_specs=[query_spec, query_spec],
    )
    return pl.pallas_call(
        attention_kernel,
        grid_spec=grid_spec,
        out_shape=[
            jax.ShapeDtypeStruct((tokens, width), jnp.float32),
            jax.ShapeDtypeStruct((tokens, width), jnp.float32),
        ],
        compiler_params=pltpu.CompilerParams(
            dimension_semantics=("arbitrary", "arbitrary"),
        ),
    )(first_block, last_block, sample_ends, q, dq, k, dk, v, dv)


def per_device(
    q_proj, q_tangent, k_proj, k_tangent, v_proj, v_tangent, query_norm_gain, key_norm_gain, lengths
):
    q_normed, dq_normed = normalize(q_proj, q_tangent, query_norm_gain)
    k_normed, dk_normed = normalize(k_proj, k_tangent, key_norm_gain)
    seq_count = lax.axis_size("seq")
    tokens = q_proj.shape[1]
    width = q_proj.shape[2]
    local_heads = width // HEAD_DIM // seq_count
    pack_tokens = tokens * seq_count

    def to_heads(array):
        moved = lax.all_to_all(
            array.reshape(1, tokens, seq_count, local_heads, HEAD_DIM),
            "seq", split_axis=2, concat_axis=1, tiled=True,
        )
        return moved.reshape(pack_tokens, local_heads * HEAD_DIM)

    own_row = lax.dynamic_slice_in_dim(lengths, lax.axis_index("samp"), 1, 0)[0]
    first_block, last_block, sample_ends = block_tables(own_row, pack_tokens)
    output, tangent = attend(
        to_heads(q_normed), to_heads(dq_normed), to_heads(k_normed), to_heads(dk_normed),
        to_heads(v_proj), to_heads(v_tangent), first_block, last_block, sample_ends,
    )

    def to_tokens(array):
        moved = lax.all_to_all(
            array.reshape(1, pack_tokens, 1, local_heads, HEAD_DIM),
            "seq", split_axis=1, concat_axis=2, tiled=True,
        )
        return moved.reshape(1, tokens, width)

    return (to_tokens(output), to_tokens(tangent))


def solution(mesh):
    placed = (
        P(("groups", "samp"), "seq", None),
        P(("groups", "samp"), "seq", None),
        P(("groups", "samp"), "seq", None),
        P(("groups", "samp"), "seq", None),
        P(("groups", "samp"), "seq", None),
        P(("groups", "samp"), "seq", None),
        P(),
        P(),
        P("groups", None),
    )
    return jax.shard_map(
        per_device,
        mesh=mesh,
        in_specs=placed,
        out_specs=(P(("groups", "samp"), "seq", None), P(("groups", "samp"), "seq", None)),
        check_vma=False,
    )
```

```python
import functools
import math

import jax
import jax.numpy as jnp
from jax import lax
from jax.experimental import pallas as pl
from jax.experimental.pallas import tpu as pltpu
from jax.sharding import PartitionSpec as P

HEAD_DIM = 128
BLOCK = 256


def normalize(source, source_tangent, gain):
    widened = source.astype(jnp.float32)
    dwidened = source_tangent.astype(jnp.float32)
    inverse = lax.rsqrt(jnp.mean(widened * widened, axis=-1, keepdims=True) + 1e-06)
    radial = jnp.mean(widened * dwidened, axis=-1, keepdims=True)
    normed = (widened * inverse * gain).astype(jnp.bfloat16)
    tangent = ((dwidened * inverse - widened * inverse**3 * radial) * gain).astype(jnp.bfloat16)
    return (normed, tangent)


def block_tables(sample_lengths, count):
    sample_ends = jnp.cumsum(sample_lengths).astype(jnp.int32)
    sample_starts = sample_ends - sample_lengths
    blocks = count // BLOCK
    first_rows = jnp.arange(blocks, dtype=jnp.int32) * BLOCK
    last_rows = first_rows + (BLOCK - 1)
    first_segment = jnp.sum((first_rows[:, None] >= sample_ends[None, :]).astype(jnp.int32), axis=1)
    last_segment = jnp.sum((last_rows[:, None] >= sample_ends[None, :]).astype(jnp.int32), axis=1)
    samples = sample_lengths.shape[0]
    first_segment = jnp.clip(first_segment, 0, samples - 1)
    last_segment = jnp.clip(last_segment, 0, samples - 1)
    first_key = jnp.take(sample_starts, first_segment)
    last_key = jnp.take(sample_ends, last_segment)
    first_block = jnp.clip(first_key // BLOCK, 0, blocks - 1)
    last_block = jnp.clip((last_key - 1) // BLOCK + 1, first_block + 1, blocks)
    return first_block.astype(jnp.int32), last_block.astype(jnp.int32), sample_ends


def attention_kernel(
    first_ref, last_ref, ends_ref,
    q_ref, dq_ref, k_ref, dk_ref, v_ref, dv_ref,
    result_ref,
):
    i = pl.program_id(1)
    samples = ends_ref.shape[0]
    factor = 1.0 / math.sqrt(HEAD_DIM)
    queries = q_ref[...]
    dqueries = dq_ref[...]
    both_queries = jnp.concatenate([dqueries, queries], axis=1)

    def segment_of(positions):
        seg = jnp.zeros(positions.shape, jnp.int32)
        for j in range(samples):
            seg = seg + (positions >= ends_ref[j]).astype(jnp.int32)
        return seg

    query_positions = i * BLOCK + lax.broadcasted_iota(jnp.int32, (BLOCK, 1), 0)
    query_segment = segment_of(query_positions)
    first = first_ref[i]
    last = last_ref[i]

    def scores_of(kb):
        start = pl.multiple_of(kb * BLOCK, BLOCK)
        key_rows = k_ref[pl.ds(start, BLOCK), :]
        key_positions = start + lax.broadcasted_iota(jnp.int32, (1, BLOCK), 1)
        same = query_segment == segment_of(key_positions)
        raw = lax.dot_general(
            queries, key_rows, (((1,), (1,)), ((), ())), preferred_element_type=jnp.float32
        ) * factor
        return raw, same, start, key_rows

    def statistics(kb, carry):
        row_top, total = carry
        raw, same, _, _ = scores_of(kb)
        masked = jnp.where(same, raw, -1e30)
        new_top = jnp.maximum(row_top, jnp.max(masked, axis=1, keepdims=True))
        exponent = jnp.where(same, jnp.exp(masked - new_top), 0.0)
        total = total * jnp.exp(row_top - new_top) + jnp.sum(exponent, axis=1, keepdims=True)
        return new_top, total

    row_top, total = lax.fori_loop(
        first, last, statistics,
        (jnp.full((BLOCK, 1), -1e30, jnp.float32), jnp.zeros((BLOCK, 1), jnp.float32)),
    )
    inverse_total = 1.0 / total

    def sums(kb, carry):
        center, output, spread_sum, dvalue_sum = carry
        raw, same, start, key_rows = scores_of(kb)
        dkey_rows = dk_ref[pl.ds(start, BLOCK), :]
        value_rows = v_ref[pl.ds(start, BLOCK), :]
        dvalue_rows = dv_ref[pl.ds(start, BLOCK), :]
        both_keys = jnp.concatenate([key_rows, dkey_rows], axis=1)
        dscores = lax.dot_general(
            both_queries, both_keys, (((1,), (1,)), ((), ())), preferred_element_type=jnp.float32
        ) * factor
        weights = jnp.where(same, jnp.exp(raw - row_top), 0.0) * inverse_total
        product = jnp.where(same, weights * dscores, 0.0)
        center = center + jnp.sum(product, axis=1, keepdims=True)
        rounded = weights.astype(jnp.bfloat16)
        spread = product.astype(jnp.bfloat16)
        output = output + jnp.dot(rounded, value_rows, preferred_element_type=jnp.float32)
        spread_sum = spread_sum + jnp.dot(spread, value_rows, preferred_element_type=jnp.float32)
        dvalue_sum = dvalue_sum + jnp.dot(rounded, dvalue_rows, preferred_element_type=jnp.float32)
        return center, output, spread_sum, dvalue_sum

    empty = jnp.zeros((BLOCK, HEAD_DIM), jnp.float32)
    center, output, spread_sum, dvalue_sum = lax.fori_loop(
        first, last, sums, (jnp.zeros((BLOCK, 1), jnp.float32), empty, empty, empty)
    )
    result_ref[:, :HEAD_DIM] = output.astype(result_ref.dtype)
    result_ref[:, HEAD_DIM:] = (spread_sum - center * output + dvalue_sum).astype(result_ref.dtype)


def attend(stacked, heads, first_block, last_block, sample_ends, result_dtype):
    tokens = stacked.shape[0]
    blocks = tokens // BLOCK

    def query_spec(t):
        return pl.BlockSpec((BLOCK, HEAD_DIM), lambda h, i, *_: (i, t * heads + h))

    def key_spec(t):
        return pl.BlockSpec((tokens, HEAD_DIM), lambda h, i, *_: (0, t * heads + h))

    grid_spec = pltpu.PrefetchScalarGridSpec(
        num_scalar_prefetch=3,
        grid=(heads, blocks),
        in_specs=[query_spec(0), query_spec(1), key_spec(2), key_spec(3), key_spec(4), key_spec(5)],
        out_specs=pl.BlockSpec((BLOCK, 2 * HEAD_DIM), lambda h, i, *_: (i, h)),
    )
    return pl.pallas_call(
        attention_kernel,
        grid_spec=grid_spec,
        out_shape=jax.ShapeDtypeStruct((tokens, heads * 2 * HEAD_DIM), result_dtype),
        compiler_params=pltpu.CompilerParams(
            dimension_semantics=("arbitrary", "arbitrary"),
        ),
    )(first_block, last_block, sample_ends, stacked, stacked, stacked, stacked, stacked, stacked)


CHUNKS = 4
RESULT_DTYPE = jnp.float32


def per_device(
    q_proj, q_tangent, k_proj, k_tangent, v_proj, v_tangent, query_norm_gain, key_norm_gain, lengths
):
    q_normed, dq_normed = normalize(q_proj, q_tangent, query_norm_gain)
    k_normed, dk_normed = normalize(k_proj, k_tangent, key_norm_gain)
    seq_count = lax.axis_size("seq")
    tokens = q_proj.shape[1]
    width = q_proj.shape[2]
    local_heads = width // HEAD_DIM // seq_count
    pack_tokens = tokens * seq_count
    chunks = min(CHUNKS, local_heads)
    chunk_heads = local_heads // chunks

    own_row = lax.dynamic_slice_in_dim(lengths, lax.axis_index("samp"), 1, 0)[0]
    first_block, last_block, sample_ends = block_tables(own_row, pack_tokens)
    split = [
        array.reshape(1, tokens, seq_count, local_heads, HEAD_DIM)
        for array in (q_normed, dq_normed, k_normed, dk_normed, v_proj, v_tangent)
    ]
    results = []
    for c in range(chunks):
        heads = slice(c * chunk_heads, (c + 1) * chunk_heads)
        payload = jnp.stack([array[:, :, :, heads] for array in split], axis=3)
        moved = lax.all_to_all(payload, "seq", split_axis=2, concat_axis=1, tiled=True)
        stacked = moved.reshape(pack_tokens, 6 * chunk_heads * HEAD_DIM)
        result = attend(stacked, chunk_heads, first_block, last_block, sample_ends, RESULT_DTYPE)
        back = lax.all_to_all(
            result.reshape(1, pack_tokens, 1, chunk_heads, 2, HEAD_DIM),
            "seq", split_axis=1, concat_axis=2, tiled=True,
        )
        results.append(back)
    joined = jnp.concatenate(results, axis=3).astype(jnp.float32)
    output = joined[:, :, :, :, 0].reshape(1, tokens, width)
    tangent = joined[:, :, :, :, 1].reshape(1, tokens, width)
    return (output, tangent)


def solution(mesh):
    placed = (
        P(("groups", "samp"), "seq", None),
        P(("groups", "samp"), "seq", None),
        P(("groups", "samp"), "seq", None),
        P(("groups", "samp"), "seq", None),
        P(("groups", "samp"), "seq", None),
        P(("groups", "samp"), "seq", None),
        P(),
        P(),
        P("groups", None),
    )
    return jax.shard_map(
        per_device,
        mesh=mesh,
        in_specs=placed,
        out_specs=(P(("groups", "samp"), "seq", None), P(("groups", "samp"), "seq", None)),
        check_vma=False,
    )
```

```python
import functools
import math

import jax
import jax.numpy as jnp
from jax import lax
from jax.experimental import pallas as pl
from jax.experimental.pallas import tpu as pltpu
from jax.sharding import PartitionSpec as P

HEAD_DIM = 128
BLOCK = 256
KEY_BLOCK = 128


def normalize(source, source_tangent, gain):
    widened = source.astype(jnp.float32)
    dwidened = source_tangent.astype(jnp.float32)
    inverse = lax.rsqrt(jnp.mean(widened * widened, axis=-1, keepdims=True) + 1e-06)
    radial = jnp.mean(widened * dwidened, axis=-1, keepdims=True)
    normed = (widened * inverse * gain).astype(jnp.bfloat16)
    tangent = ((dwidened * inverse - widened * inverse**3 * radial) * gain).astype(jnp.bfloat16)
    return (normed, tangent)


def block_tables(sample_lengths, count):
    sample_ends = jnp.cumsum(sample_lengths).astype(jnp.int32)
    sample_starts = sample_ends - sample_lengths
    blocks = count // BLOCK
    first_rows = jnp.arange(blocks, dtype=jnp.int32) * BLOCK
    last_rows = first_rows + (BLOCK - 1)
    first_segment = jnp.sum((first_rows[:, None] >= sample_ends[None, :]).astype(jnp.int32), axis=1)
    last_segment = jnp.sum((last_rows[:, None] >= sample_ends[None, :]).astype(jnp.int32), axis=1)
    samples = sample_lengths.shape[0]
    first_segment = jnp.clip(first_segment, 0, samples - 1)
    last_segment = jnp.clip(last_segment, 0, samples - 1)
    first_key = jnp.take(sample_starts, first_segment)
    last_key = jnp.take(sample_ends, last_segment)
    key_blocks = count // KEY_BLOCK
    first_block = jnp.clip(first_key // KEY_BLOCK, 0, key_blocks - 1)
    last_block = jnp.clip((last_key - 1) // KEY_BLOCK + 1, first_block + 1, key_blocks)
    return first_block.astype(jnp.int32), last_block.astype(jnp.int32), sample_ends


def attention_kernel(
    first_ref, last_ref, ends_ref,
    q_ref, dq_ref, k_ref, dk_ref, v_ref, dv_ref,
    result_ref,
):
    i = pl.program_id(1)
    samples = ends_ref.shape[0]
    factor = 1.0 / math.sqrt(HEAD_DIM)
    queries = q_ref[...]
    dqueries = dq_ref[...]
    both_queries = jnp.concatenate([dqueries, queries], axis=1)

    def segment_of(positions):
        seg = jnp.zeros(positions.shape, jnp.int32)
        for j in range(samples):
            seg = seg + (positions >= ends_ref[j]).astype(jnp.int32)
        return seg

    query_positions = i * BLOCK + lax.broadcasted_iota(jnp.int32, (BLOCK, 1), 0)
    query_segment = segment_of(query_positions)
    first = first_ref[i]
    last = last_ref[i]

    def scores_of(kb):
        start = pl.multiple_of(kb * KEY_BLOCK, KEY_BLOCK)
        key_rows = k_ref[pl.ds(start, KEY_BLOCK), :]
        key_positions = start + lax.broadcasted_iota(jnp.int32, (1, KEY_BLOCK), 1)
        same = query_segment == segment_of(key_positions)
        raw = lax.dot_general(
            queries, key_rows, (((1,), (1,)), ((), ())), preferred_element_type=jnp.float32
        ) * factor
        return raw, same, start, key_rows

    def statistics(kb, carry):
        row_top, total = carry
        raw, same, _, _ = scores_of(kb)
        masked = jnp.where(same, raw, -1e30)
        new_top = jnp.maximum(row_top, jnp.max(masked, axis=1, keepdims=True))
        exponent = jnp.where(same, jnp.exp(masked - new_top), 0.0)
        total = total * jnp.exp(row_top - new_top) + jnp.sum(exponent, axis=1, keepdims=True)
        return new_top, total

    row_top, total = lax.fori_loop(
        first, last, statistics,
        (jnp.full((BLOCK, 1), -1e30, jnp.float32), jnp.zeros((BLOCK, 1), jnp.float32)),
    )
    inverse_total = 1.0 / total

    def sums(kb, carry):
        center, output, spread_sum, dvalue_sum = carry
        raw, same, start, key_rows = scores_of(kb)
        dkey_rows = dk_ref[pl.ds(start, KEY_BLOCK), :]
        value_rows = v_ref[pl.ds(start, KEY_BLOCK), :]
        dvalue_rows = dv_ref[pl.ds(start, KEY_BLOCK), :]
        both_keys = jnp.concatenate([key_rows, dkey_rows], axis=1)
        dscores = lax.dot_general(
            both_queries, both_keys, (((1,), (1,)), ((), ())), preferred_element_type=jnp.float32
        ) * factor
        weights = jnp.where(same, jnp.exp(raw - row_top), 0.0) * inverse_total
        product = jnp.where(same, weights * dscores, 0.0)
        center = center + jnp.sum(product, axis=1, keepdims=True)
        rounded = weights.astype(jnp.bfloat16)
        spread = product.astype(jnp.bfloat16)
        output = output + jnp.dot(rounded, value_rows, preferred_element_type=jnp.float32)
        spread_sum = spread_sum + jnp.dot(spread, value_rows, preferred_element_type=jnp.float32)
        dvalue_sum = dvalue_sum + jnp.dot(rounded, dvalue_rows, preferred_element_type=jnp.float32)
        return center, output, spread_sum, dvalue_sum

    empty = jnp.zeros((BLOCK, HEAD_DIM), jnp.float32)
    center, output, spread_sum, dvalue_sum = lax.fori_loop(
        first, last, sums, (jnp.zeros((BLOCK, 1), jnp.float32), empty, empty, empty)
    )
    result_ref[0] = output.astype(result_ref.dtype)
    result_ref[1] = (spread_sum - center * output + dvalue_sum).astype(result_ref.dtype)


def attend(stacked, heads, first_block, last_block, sample_ends, result_dtype):
    tokens = stacked.shape[0]
    blocks = tokens // BLOCK

    def query_spec(t):
        return pl.BlockSpec((BLOCK, HEAD_DIM), lambda h, i, *_: (i, t * heads + h))

    def key_spec(t):
        return pl.BlockSpec((tokens, HEAD_DIM), lambda h, i, *_: (0, t * heads + h))

    grid_spec = pltpu.PrefetchScalarGridSpec(
        num_scalar_prefetch=3,
        grid=(heads, blocks),
        in_specs=[query_spec(0), query_spec(1), key_spec(2), key_spec(3), key_spec(4), key_spec(5)],
        out_specs=pl.BlockSpec((2, BLOCK, HEAD_DIM), lambda h, i, *_: (0, i, h)),
    )
    return pl.pallas_call(
        attention_kernel,
        grid_spec=grid_spec,
        out_shape=jax.ShapeDtypeStruct((2, tokens, heads * HEAD_DIM), result_dtype),
        compiler_params=pltpu.CompilerParams(
            dimension_semantics=("arbitrary", "arbitrary"),
        ),
    )(first_block, last_block, sample_ends, stacked, stacked, stacked, stacked, stacked, stacked)


CHUNKS = 4
RESULT_DTYPE = jnp.bfloat16


def per_device(
    q_proj, q_tangent, k_proj, k_tangent, v_proj, v_tangent, query_norm_gain, key_norm_gain, lengths
):
    q_normed, dq_normed = normalize(q_proj, q_tangent, query_norm_gain)
    k_normed, dk_normed = normalize(k_proj, k_tangent, key_norm_gain)
    seq_count = lax.axis_size("seq")
    tokens = q_proj.shape[1]
    width = q_proj.shape[2]
    local_heads = width // HEAD_DIM // seq_count
    pack_tokens = tokens * seq_count
    chunks = min(CHUNKS, local_heads)
    chunk_heads = local_heads // chunks

    own_row = lax.dynamic_slice_in_dim(lengths, lax.axis_index("samp"), 1, 0)[0]
    first_block, last_block, sample_ends = block_tables(own_row, pack_tokens)
    split = [
        array.reshape(1, tokens, seq_count, local_heads, HEAD_DIM)
        for array in (q_normed, dq_normed, k_normed, dk_normed, v_proj, v_tangent)
    ]
    results = []
    for c in range(chunks):
        heads = slice(c * chunk_heads, (c + 1) * chunk_heads)
        payload = jnp.stack([array[:, :, :, heads] for array in split], axis=3)
        moved = lax.all_to_all(payload, "seq", split_axis=2, concat_axis=1, tiled=True)
        stacked = moved.reshape(pack_tokens, 6 * chunk_heads * HEAD_DIM)
        result = attend(stacked, chunk_heads, first_block, last_block, sample_ends, RESULT_DTYPE)
        back = lax.all_to_all(
            result.reshape(2, seq_count, tokens, chunk_heads * HEAD_DIM),
            "seq", split_axis=1, concat_axis=1, tiled=True,
        )
        results.append(back)
    joined = jnp.concatenate(results, axis=3)
    joined = jnp.swapaxes(joined, 1, 2).reshape(2, 1, tokens, width).astype(jnp.float32)
    return (joined[0], joined[1])


def solution(mesh):
    placed = (
        P(("groups", "samp"), "seq", None),
        P(("groups", "samp"), "seq", None),
        P(("groups", "samp"), "seq", None),
        P(("groups", "samp"), "seq", None),
        P(("groups", "samp"), "seq", None),
        P(("groups", "samp"), "seq", None),
        P(),
        P(),
        P("groups", None),
    )
    return jax.shard_map(
        per_device,
        mesh=mesh,
        in_specs=placed,
        out_specs=(P(("groups", "samp"), "seq", None), P(("groups", "samp"), "seq", None)),
        check_vma=False,
    )
```

```python
import math

import jax
import jax.numpy as jnp
from jax import lax
from jax.experimental import pallas as pl
from jax.experimental.pallas import tpu as pltpu
from jax.sharding import PartitionSpec as P


HEAD_DIM = 128
BLOCK = 256
KEY_BLOCK = 256


def normalize(source, source_tangent, gain):
    widened = source.astype(jnp.float32)
    dwidened = source_tangent.astype(jnp.float32)
    inverse = lax.rsqrt(jnp.mean(widened * widened, axis=-1, keepdims=True) + 1e-06)
    radial = jnp.mean(widened * dwidened, axis=-1, keepdims=True)
    normed = (widened * inverse * gain).astype(jnp.bfloat16)
    tangent = ((dwidened * inverse - widened * inverse**3 * radial) * gain).astype(jnp.bfloat16)
    return (normed, tangent)


def block_tables(sample_lengths, count):
    sample_ends = jnp.cumsum(sample_lengths).astype(jnp.int32)
    sample_starts = sample_ends - sample_lengths
    blocks = count // BLOCK
    first_rows = jnp.arange(blocks, dtype=jnp.int32) * BLOCK
    last_rows = first_rows + (BLOCK - 1)
    first_segment = jnp.sum((first_rows[:, None] >= sample_ends[None, :]).astype(jnp.int32), axis=1)
    last_segment = jnp.sum((last_rows[:, None] >= sample_ends[None, :]).astype(jnp.int32), axis=1)
    samples = sample_lengths.shape[0]
    first_segment = jnp.clip(first_segment, 0, samples - 1)
    last_segment = jnp.clip(last_segment, 0, samples - 1)
    first_key = jnp.take(sample_starts, first_segment)
    last_key = jnp.take(sample_ends, last_segment)
    key_blocks = count // KEY_BLOCK
    first_block = jnp.clip(first_key // KEY_BLOCK, 0, key_blocks - 1)
    last_block = jnp.clip((last_key - 1) // KEY_BLOCK + 1, first_block + 1, key_blocks)
    return first_block.astype(jnp.int32), last_block.astype(jnp.int32), sample_ends


def attention_kernel(
    first_ref, last_ref, ends_ref,
    q_ref, dq_ref, k_ref, dk_ref, v_ref, dv_ref,
    result_ref,
):
    i = pl.program_id(1)
    samples = ends_ref.shape[0]
    factor = 1.0 / math.sqrt(HEAD_DIM)
    queries = q_ref[...]
    dqueries = dq_ref[...]
    both_queries = jnp.concatenate([dqueries, queries], axis=1)

    def segment_of(positions):
        seg = jnp.zeros(positions.shape, jnp.int32)
        for j in range(samples):
            seg = seg + (positions >= ends_ref[j]).astype(jnp.int32)
        return seg

    query_positions = i * BLOCK + lax.broadcasted_iota(jnp.int32, (BLOCK, 1), 0)
    query_segment = segment_of(query_positions)
    first = first_ref[i]
    last = last_ref[i]

    def scores_of(kb):
        start = pl.multiple_of(kb * KEY_BLOCK, KEY_BLOCK)
        key_rows = k_ref[pl.ds(start, KEY_BLOCK), :]
        key_positions = start + lax.broadcasted_iota(jnp.int32, (1, KEY_BLOCK), 1)
        same = query_segment == segment_of(key_positions)
        raw = lax.dot_general(
            queries, key_rows, (((1,), (1,)), ((), ())), preferred_element_type=jnp.float32
        ) * factor
        return raw, same, start, key_rows

    def statistics(kb, carry):
        row_top, total = carry
        raw, same, _, _ = scores_of(kb)
        masked = jnp.where(same, raw, -1e30)
        new_top = jnp.maximum(row_top, jnp.max(masked, axis=1, keepdims=True))
        exponent = jnp.where(same, jnp.exp(masked - new_top), 0.0)
        total = total * jnp.exp(row_top - new_top) + jnp.sum(exponent, axis=1, keepdims=True)
        return new_top, total

    row_top, total = lax.fori_loop(
        first, last, statistics,
        (jnp.full((BLOCK, 1), -1e30, jnp.float32), jnp.zeros((BLOCK, 1), jnp.float32)),
    )
    inverse_total = 1.0 / total

    def sums(kb, carry):
        center, output, spread_sum, dvalue_sum = carry
        raw, same, start, key_rows = scores_of(kb)
        dkey_rows = dk_ref[pl.ds(start, KEY_BLOCK), :]
        value_rows = v_ref[pl.ds(start, KEY_BLOCK), :]
        dvalue_rows = dv_ref[pl.ds(start, KEY_BLOCK), :]
        both_keys = jnp.concatenate([key_rows, dkey_rows], axis=1)
        dscores = lax.dot_general(
            both_queries, both_keys, (((1,), (1,)), ((), ())), preferred_element_type=jnp.float32
        ) * factor
        weights = jnp.where(same, jnp.exp(raw - row_top), 0.0) * inverse_total
        product = jnp.where(same, weights * dscores, 0.0)
        center = center + jnp.sum(product, axis=1, keepdims=True)
        rounded = weights.astype(jnp.bfloat16)
        spread = product.astype(jnp.bfloat16)
        output = output + jnp.dot(rounded, value_rows, preferred_element_type=jnp.float32)
        spread_sum = spread_sum + jnp.dot(spread, value_rows, preferred_element_type=jnp.float32)
        dvalue_sum = dvalue_sum + jnp.dot(rounded, dvalue_rows, preferred_element_type=jnp.float32)
        return center, output, spread_sum, dvalue_sum

    empty = jnp.zeros((BLOCK, HEAD_DIM), jnp.float32)
    center, output, spread_sum, dvalue_sum = lax.fori_loop(
        first, last, sums, (jnp.zeros((BLOCK, 1), jnp.float32), empty, empty, empty)
    )
    result_ref[0] = output.astype(result_ref.dtype)
    result_ref[1] = (spread_sum - center * output + dvalue_sum).astype(result_ref.dtype)


def attend(stacked, heads, first_block, last_block, sample_ends, result_dtype):
    tokens = stacked.shape[0]
    blocks = tokens // BLOCK

    def query_spec(t):
        return pl.BlockSpec((BLOCK, HEAD_DIM), lambda h, i, *_: (i, t * heads + h))

    def key_spec(t):
        return pl.BlockSpec((tokens, HEAD_DIM), lambda h, i, *_: (0, t * heads + h))

    grid_spec = pltpu.PrefetchScalarGridSpec(
        num_scalar_prefetch=3,
        grid=(heads, blocks),
        in_specs=[query_spec(0), query_spec(1), key_spec(2), key_spec(3), key_spec(4), key_spec(5)],
        out_specs=pl.BlockSpec((2, BLOCK, HEAD_DIM), lambda h, i, *_: (0, i, h)),
    )
    return pl.pallas_call(
        attention_kernel,
        grid_spec=grid_spec,
        out_shape=jax.ShapeDtypeStruct((2, tokens, heads * HEAD_DIM), result_dtype),
        compiler_params=pltpu.CompilerParams(
            dimension_semantics=("arbitrary", "arbitrary"),
        ),
    )(first_block, last_block, sample_ends, stacked, stacked, stacked, stacked, stacked, stacked)


CHUNKS = 4
RESULT_DTYPE = jnp.bfloat16


def per_device_body(
    q_proj, q_tangent, k_proj, k_tangent, v_proj, v_tangent, query_norm_gain, key_norm_gain, lengths
):
    q_normed, dq_normed = normalize(q_proj, q_tangent, query_norm_gain)
    k_normed, dk_normed = normalize(k_proj, k_tangent, key_norm_gain)
    seq_count = lax.axis_size("seq")
    tokens = q_proj.shape[1]
    width = q_proj.shape[2]
    local_heads = width // HEAD_DIM // seq_count
    pack_tokens = tokens * seq_count
    chunks = min(CHUNKS, local_heads)
    chunk_heads = local_heads // chunks

    own_row = lax.dynamic_slice_in_dim(lengths, lax.axis_index("samp"), 1, 0)[0]
    first_block, last_block, sample_ends = block_tables(own_row, pack_tokens)
    split = [
        array.reshape(1, tokens, seq_count, local_heads, HEAD_DIM)
        for array in (q_normed, dq_normed, k_normed, dk_normed, v_proj, v_tangent)
    ]
    results = []
    for c in range(chunks):
        heads = slice(c * chunk_heads, (c + 1) * chunk_heads)
        payload = jnp.stack([array[:, :, :, heads] for array in split], axis=3)
        moved = lax.all_to_all(payload, "seq", split_axis=2, concat_axis=1, tiled=True)
        stacked = moved.reshape(pack_tokens, 6 * chunk_heads * HEAD_DIM)
        result = attend(stacked, chunk_heads, first_block, last_block, sample_ends, RESULT_DTYPE)
        back = lax.all_to_all(
            result.reshape(2, seq_count, tokens, chunk_heads * HEAD_DIM),
            "seq", split_axis=1, concat_axis=1, tiled=True,
        )
        results.append(back)
    joined = jnp.concatenate(results, axis=3)
    joined = jnp.swapaxes(joined, 1, 2).reshape(2, 1, tokens, width).astype(jnp.float32)
    return (joined[0], joined[1])


def solution(mesh):
    placed = (
        P(("groups", "samp"), "seq", None),
        P(("groups", "samp"), "seq", None),
        P(("groups", "samp"), "seq", None),
        P(("groups", "samp"), "seq", None),
        P(("groups", "samp"), "seq", None),
        P(("groups", "samp"), "seq", None),
        P(),
        P(),
        P("groups", None),
    )
    return jax.shard_map(
        per_device_body,
        mesh=mesh,
        in_specs=placed,
        out_specs=(P(("groups", "samp"), "seq", None), P(("groups", "samp"), "seq", None)),
        check_vma=False,
    )
```

```python
import math

import jax
import jax.numpy as jnp
from jax import lax
from jax.experimental import pallas as pl
from jax.experimental.pallas import tpu as pltpu
from jax.sharding import PartitionSpec as P


HEAD_DIM = 128
BLOCK = 256
KEY_BLOCK = 256


def normalize(source, source_tangent, gain):
    widened = source.astype(jnp.float32)
    dwidened = source_tangent.astype(jnp.float32)
    inverse = lax.rsqrt(jnp.mean(widened * widened, axis=-1, keepdims=True) + 1e-06)
    radial = jnp.mean(widened * dwidened, axis=-1, keepdims=True)
    normed = (widened * inverse * gain).astype(jnp.bfloat16)
    tangent = ((dwidened * inverse - widened * inverse**3 * radial) * gain).astype(jnp.bfloat16)
    return (normed, tangent)


def block_tables(sample_lengths, count):
    sample_ends = jnp.cumsum(sample_lengths).astype(jnp.int32)
    sample_starts = sample_ends - sample_lengths
    blocks = count // BLOCK
    first_rows = jnp.arange(blocks, dtype=jnp.int32) * BLOCK
    last_rows = first_rows + (BLOCK - 1)
    first_segment = jnp.sum((first_rows[:, None] >= sample_ends[None, :]).astype(jnp.int32), axis=1)
    last_segment = jnp.sum((last_rows[:, None] >= sample_ends[None, :]).astype(jnp.int32), axis=1)
    samples = sample_lengths.shape[0]
    first_segment = jnp.clip(first_segment, 0, samples - 1)
    last_segment = jnp.clip(last_segment, 0, samples - 1)
    first_key = jnp.take(sample_starts, first_segment)
    last_key = jnp.take(sample_ends, last_segment)
    key_blocks = count // KEY_BLOCK
    first_block = jnp.clip(first_key // KEY_BLOCK, 0, key_blocks - 1)
    last_block = jnp.clip((last_key - 1) // KEY_BLOCK + 1, first_block + 1, key_blocks)
    return first_block.astype(jnp.int32), last_block.astype(jnp.int32), sample_ends


def attention_kernel(
    first_ref, last_ref, ends_ref,
    q_ref, dq_ref, k_ref, dk_ref, v_ref, dv_ref,
    result_ref,
):
    i = pl.program_id(1)
    samples = ends_ref.shape[0]
    factor = 1.0 / math.sqrt(HEAD_DIM)
    queries = q_ref[...]
    dqueries = dq_ref[...]
    both_queries = jnp.concatenate([dqueries, queries], axis=1)

    def segment_of(positions):
        seg = jnp.zeros(positions.shape, jnp.int32)
        for j in range(samples):
            seg = seg + (positions >= ends_ref[j]).astype(jnp.int32)
        return seg

    query_positions = i * BLOCK + lax.broadcasted_iota(jnp.int32, (BLOCK, 1), 0)
    query_segment = segment_of(query_positions)
    first = first_ref[i]
    last = last_ref[i]

    def scores_of(kb):
        start = pl.multiple_of(kb * KEY_BLOCK, KEY_BLOCK)
        key_rows = k_ref[pl.ds(start, KEY_BLOCK), :]
        key_positions = start + lax.broadcasted_iota(jnp.int32, (1, KEY_BLOCK), 1)
        same = query_segment == segment_of(key_positions)
        raw = lax.dot_general(
            queries, key_rows, (((1,), (1,)), ((), ())), preferred_element_type=jnp.float32
        ) * factor
        return raw, same, start, key_rows

    def statistics(kb, carry):
        row_top, total = carry
        raw, same, _, _ = scores_of(kb)
        masked = jnp.where(same, raw, -1e30)
        new_top = jnp.maximum(row_top, jnp.max(masked, axis=1, keepdims=True))
        exponent = jnp.where(same, jnp.exp(masked - new_top), 0.0)
        total = total * jnp.exp(row_top - new_top) + jnp.sum(exponent, axis=1, keepdims=True)
        return new_top, total

    row_top, total = lax.fori_loop(
        first, last, statistics,
        (jnp.full((BLOCK, 1), -1e30, jnp.float32), jnp.zeros((BLOCK, 1), jnp.float32)),
    )
    inverse_total = 1.0 / total

    def sums(kb, carry):
        center, output, spread_sum, dvalue_sum = carry
        raw, same, start, key_rows = scores_of(kb)
        dkey_rows = dk_ref[pl.ds(start, KEY_BLOCK), :]
        value_rows = v_ref[pl.ds(start, KEY_BLOCK), :]
        dvalue_rows = dv_ref[pl.ds(start, KEY_BLOCK), :]
        both_keys = jnp.concatenate([key_rows, dkey_rows], axis=1)
        dscores = lax.dot_general(
            both_queries, both_keys, (((1,), (1,)), ((), ())), preferred_element_type=jnp.float32
        ) * factor
        weights = jnp.where(same, jnp.exp(raw - row_top), 0.0) * inverse_total
        product = jnp.where(same, weights * dscores, 0.0)
        center = center + jnp.sum(product, axis=1, keepdims=True)
        rounded = weights.astype(jnp.bfloat16)
        spread = product.astype(jnp.bfloat16)
        output = output + jnp.dot(rounded, value_rows, preferred_element_type=jnp.float32)
        spread_sum = spread_sum + jnp.dot(spread, value_rows, preferred_element_type=jnp.float32)
        dvalue_sum = dvalue_sum + jnp.dot(rounded, dvalue_rows, preferred_element_type=jnp.float32)
        return center, output, spread_sum, dvalue_sum

    empty = jnp.zeros((BLOCK, HEAD_DIM), jnp.float32)
    center, output, spread_sum, dvalue_sum = lax.fori_loop(
        first, last, sums, (jnp.zeros((BLOCK, 1), jnp.float32), empty, empty, empty)
    )
    result_ref[0] = output.astype(result_ref.dtype)
    result_ref[1] = (spread_sum - center * output + dvalue_sum).astype(result_ref.dtype)


def attend(stacked, values, heads, offset, first_block, last_block, sample_ends, result_dtype):
    tokens = stacked.shape[0]
    all_heads = values.shape[1] // (2 * HEAD_DIM)
    blocks = tokens // BLOCK

    def query_spec(t):
        return pl.BlockSpec((BLOCK, HEAD_DIM), lambda h, i, *_: (i, t * heads + h))

    def key_spec(t):
        return pl.BlockSpec((tokens, HEAD_DIM), lambda h, i, *_: (0, t * heads + h))

    def value_spec(t):
        return pl.BlockSpec((tokens, HEAD_DIM), lambda h, i, *_: (0, t * all_heads + offset + h))

    grid_spec = pltpu.PrefetchScalarGridSpec(
        num_scalar_prefetch=3,
        grid=(heads, blocks),
        in_specs=[query_spec(0), query_spec(1), key_spec(2), key_spec(3), value_spec(0), value_spec(1)],
        out_specs=pl.BlockSpec((2, BLOCK, HEAD_DIM), lambda h, i, *_: (0, i, h)),
    )
    return pl.pallas_call(
        attention_kernel,
        grid_spec=grid_spec,
        out_shape=jax.ShapeDtypeStruct((2, tokens, heads * HEAD_DIM), result_dtype),
        compiler_params=pltpu.CompilerParams(
            dimension_semantics=("arbitrary", "arbitrary"),
        ),
    )(first_block, last_block, sample_ends, stacked, stacked, stacked, stacked, values, values)


CHUNKS = 4
RESULT_DTYPE = jnp.bfloat16


def per_device_body(
    q_proj, q_tangent, k_proj, k_tangent, v_proj, v_tangent, query_norm_gain, key_norm_gain, lengths
):
    seq_count = lax.axis_size("seq")
    tokens = q_proj.shape[1]
    width = q_proj.shape[2]
    local_heads = width // HEAD_DIM // seq_count
    pack_tokens = tokens * seq_count
    chunks = min(CHUNKS, local_heads)
    chunk_heads = local_heads // chunks

    value_payload = jnp.stack(
        [array.reshape(1, tokens, seq_count, local_heads, HEAD_DIM) for array in (v_proj, v_tangent)],
        axis=3,
    )
    values = lax.all_to_all(value_payload, "seq", split_axis=2, concat_axis=1, tiled=True)
    values = values.reshape(pack_tokens, 2 * local_heads * HEAD_DIM)

    q_normed, dq_normed = normalize(q_proj, q_tangent, query_norm_gain)
    k_normed, dk_normed = normalize(k_proj, k_tangent, key_norm_gain)
    own_row = lax.dynamic_slice_in_dim(lengths, lax.axis_index("samp"), 1, 0)[0]
    first_block, last_block, sample_ends = block_tables(own_row, pack_tokens)
    split = [
        array.reshape(1, tokens, seq_count, local_heads, HEAD_DIM)
        for array in (q_normed, dq_normed, k_normed, dk_normed)
    ]
    results = []
    for c in range(chunks):
        heads = slice(c * chunk_heads, (c + 1) * chunk_heads)
        payload = jnp.stack([array[:, :, :, heads] for array in split], axis=3)
        moved = lax.all_to_all(payload, "seq", split_axis=2, concat_axis=1, tiled=True)
        stacked = moved.reshape(pack_tokens, 4 * chunk_heads * HEAD_DIM)
        result = attend(
            stacked, values, chunk_heads, c * chunk_heads,
            first_block, last_block, sample_ends, RESULT_DTYPE,
        )
        back = lax.all_to_all(
            result.reshape(2, seq_count, tokens, chunk_heads * HEAD_DIM),
            "seq", split_axis=1, concat_axis=1, tiled=True,
        )
        results.append(back)
    joined = jnp.concatenate(results, axis=3)
    joined = jnp.swapaxes(joined, 1, 2).reshape(2, 1, tokens, width).astype(jnp.float32)
    return (joined[0], joined[1])


def solution(mesh):
    placed = (
        P(("groups", "samp"), "seq", None),
        P(("groups", "samp"), "seq", None),
        P(("groups", "samp"), "seq", None),
        P(("groups", "samp"), "seq", None),
        P(("groups", "samp"), "seq", None),
        P(("groups", "samp"), "seq", None),
        P(),
        P(),
        P("groups", None),
    )
    return jax.shard_map(
        per_device_body,
        mesh=mesh,
        in_specs=placed,
        out_specs=(P(("groups", "samp"), "seq", None), P(("groups", "samp"), "seq", None)),
        check_vma=False,
    )
```

```python
import math

import jax
import jax.numpy as jnp
from jax import lax
from jax.experimental import pallas as pl
from jax.experimental.pallas import tpu as pltpu
from jax.sharding import PartitionSpec as P


HEAD_DIM = 128
BLOCK = 256
KEY_BLOCK = 256


def normalize(source, source_tangent, gain):
    widened = source.astype(jnp.float32)
    dwidened = source_tangent.astype(jnp.float32)
    inverse = lax.rsqrt(jnp.mean(widened * widened, axis=-1, keepdims=True) + 1e-06)
    radial = jnp.mean(widened * dwidened, axis=-1, keepdims=True)
    normed = (widened * inverse * gain).astype(jnp.bfloat16)
    tangent = ((dwidened * inverse - widened * inverse**3 * radial) * gain).astype(jnp.bfloat16)
    return (normed, tangent)


def block_tables(sample_lengths, count):
    sample_ends = jnp.cumsum(sample_lengths).astype(jnp.int32)
    sample_starts = sample_ends - sample_lengths
    blocks = count // BLOCK
    first_rows = jnp.arange(blocks, dtype=jnp.int32) * BLOCK
    last_rows = first_rows + (BLOCK - 1)
    first_segment = jnp.sum((first_rows[:, None] >= sample_ends[None, :]).astype(jnp.int32), axis=1)
    last_segment = jnp.sum((last_rows[:, None] >= sample_ends[None, :]).astype(jnp.int32), axis=1)
    samples = sample_lengths.shape[0]
    first_segment = jnp.clip(first_segment, 0, samples - 1)
    last_segment = jnp.clip(last_segment, 0, samples - 1)
    first_key = jnp.take(sample_starts, first_segment)
    last_key = jnp.take(sample_ends, last_segment)
    key_blocks = count // KEY_BLOCK
    first_block = jnp.clip(first_key // KEY_BLOCK, 0, key_blocks - 1)
    last_block = jnp.clip((last_key - 1) // KEY_BLOCK + 1, first_block + 1, key_blocks)
    return first_block.astype(jnp.int32), last_block.astype(jnp.int32), sample_ends


def attention_kernel(
    first_ref, last_ref, ends_ref,
    q_ref, dq_ref, k_ref, dk_ref, v_ref, dv_ref,
    result_ref,
):
    i = pl.program_id(1)
    samples = ends_ref.shape[0]
    factor = 1.0 / math.sqrt(HEAD_DIM)
    queries = q_ref[...]
    dqueries = dq_ref[...]
    both_queries = jnp.concatenate([dqueries, queries], axis=1)

    def segment_of(positions):
        seg = jnp.zeros(positions.shape, jnp.int32)
        for j in range(samples):
            seg = seg + (positions >= ends_ref[j]).astype(jnp.int32)
        return seg

    query_positions = i * BLOCK + lax.broadcasted_iota(jnp.int32, (BLOCK, 1), 0)
    query_segment = segment_of(query_positions)
    first = first_ref[i]
    last = last_ref[i]

    def scores_of(kb):
        start = pl.multiple_of(kb * KEY_BLOCK, KEY_BLOCK)
        key_rows = k_ref[pl.ds(start, KEY_BLOCK), :]
        key_positions = start + lax.broadcasted_iota(jnp.int32, (1, KEY_BLOCK), 1)
        same = query_segment == segment_of(key_positions)
        raw = lax.dot_general(
            queries, key_rows, (((1,), (1,)), ((), ())), preferred_element_type=jnp.float32
        ) * factor
        return raw, same, start, key_rows

    def statistics(kb, carry):
        row_top, total = carry
        raw, same, _, _ = scores_of(kb)
        masked = jnp.where(same, raw, -1e30)
        new_top = jnp.maximum(row_top, jnp.max(masked, axis=1, keepdims=True))
        exponent = jnp.where(same, jnp.exp(masked - new_top), 0.0)
        total = total * jnp.exp(row_top - new_top) + jnp.sum(exponent, axis=1, keepdims=True)
        return new_top, total

    row_top, total = lax.fori_loop(
        first, last, statistics,
        (jnp.full((BLOCK, 1), -1e30, jnp.float32), jnp.zeros((BLOCK, 1), jnp.float32)),
    )
    inverse_total = 1.0 / total

    def sums(kb, carry):
        center, output, spread_sum, dvalue_sum = carry
        raw, same, start, key_rows = scores_of(kb)
        dkey_rows = dk_ref[pl.ds(start, KEY_BLOCK), :]
        value_rows = v_ref[pl.ds(start, KEY_BLOCK), :]
        dvalue_rows = dv_ref[pl.ds(start, KEY_BLOCK), :]
        both_keys = jnp.concatenate([key_rows, dkey_rows], axis=1)
        dscores = lax.dot_general(
            both_queries, both_keys, (((1,), (1,)), ((), ())), preferred_element_type=jnp.float32
        ) * factor
        weights = jnp.where(same, jnp.exp(raw - row_top), 0.0) * inverse_total
        product = jnp.where(same, weights * dscores, 0.0)
        center = center + jnp.sum(product, axis=1, keepdims=True)
        rounded = weights.astype(jnp.bfloat16)
        spread = product.astype(jnp.bfloat16)
        output = output + jnp.dot(rounded, value_rows, preferred_element_type=jnp.float32)
        spread_sum = spread_sum + jnp.dot(spread, value_rows, preferred_element_type=jnp.float32)
        dvalue_sum = dvalue_sum + jnp.dot(rounded, dvalue_rows, preferred_element_type=jnp.float32)
        return center, output, spread_sum, dvalue_sum

    empty = jnp.zeros((BLOCK, HEAD_DIM), jnp.float32)
    center, output, spread_sum, dvalue_sum = lax.fori_loop(
        first, last, sums, (jnp.zeros((BLOCK, 1), jnp.float32), empty, empty, empty)
    )
    result_ref[0] = output.astype(result_ref.dtype)
    result_ref[1] = (spread_sum - center * output + dvalue_sum).astype(result_ref.dtype)


def attend(stacked, values, heads, offset, first_block, last_block, sample_ends, result_dtype):
    tokens = stacked.shape[0]
    all_heads = values.shape[1] // (2 * HEAD_DIM)
    blocks = tokens // BLOCK

    def query_spec(t):
        return pl.BlockSpec((BLOCK, HEAD_DIM), lambda h, i, *_: (i, t * heads + h))

    def key_spec(t):
        return pl.BlockSpec((tokens, HEAD_DIM), lambda h, i, *_: (0, t * heads + h))

    def value_spec(t):
        return pl.BlockSpec((tokens, HEAD_DIM), lambda h, i, *_: (0, t * all_heads + offset + h))

    grid_spec = pltpu.PrefetchScalarGridSpec(
        num_scalar_prefetch=3,
        grid=(heads, blocks),
        in_specs=[query_spec(0), query_spec(1), key_spec(2), key_spec(3), value_spec(0), value_spec(1)],
        out_specs=pl.BlockSpec((2, BLOCK, HEAD_DIM), lambda h, i, *_: (0, i, h)),
    )
    return pl.pallas_call(
        attention_kernel,
        grid_spec=grid_spec,
        out_shape=jax.ShapeDtypeStruct((2, tokens, heads * HEAD_DIM), result_dtype),
        compiler_params=pltpu.CompilerParams(
            dimension_semantics=("arbitrary", "arbitrary"),
        ),
    )(first_block, last_block, sample_ends, stacked, stacked, stacked, stacked, values, values)


CHUNKS = 4
RESULT_DTYPE = jnp.bfloat16


def per_device_body(
    q_proj, q_tangent, k_proj, k_tangent, v_proj, v_tangent, query_norm_gain, key_norm_gain, lengths
):
    seq_count = lax.axis_size("seq")
    tokens = q_proj.shape[1]
    width = q_proj.shape[2]
    local_heads = width // HEAD_DIM // seq_count
    pack_tokens = tokens * seq_count
    chunks = min(CHUNKS, local_heads)
    chunk_heads = local_heads // chunks

    value_payload = jnp.stack(
        [array.reshape(1, tokens, seq_count, local_heads, HEAD_DIM) for array in (v_proj, v_tangent)],
        axis=3,
    )
    values = lax.all_to_all(value_payload, "seq", split_axis=2, concat_axis=1, tiled=True)
    values = values.reshape(pack_tokens, 2 * local_heads * HEAD_DIM)

    q_normed, dq_normed = normalize(q_proj, q_tangent, query_norm_gain)
    k_normed, dk_normed = normalize(k_proj, k_tangent, key_norm_gain)
    own_row = lax.dynamic_slice_in_dim(lengths, lax.axis_index("samp"), 1, 0)[0]
    first_block, last_block, sample_ends = block_tables(own_row, pack_tokens)
    split = [
        array.reshape(1, tokens, seq_count, local_heads, HEAD_DIM)
        for array in (q_normed, dq_normed, k_normed, dk_normed)
    ]
    results = []
    for c in range(chunks):
        heads = slice(c * chunk_heads, (c + 1) * chunk_heads)
        payload = jnp.stack([array[:, :, :, heads] for array in split], axis=3)
        moved = lax.all_to_all(payload, "seq", split_axis=2, concat_axis=1, tiled=True)
        stacked = moved.reshape(pack_tokens, 4 * chunk_heads * HEAD_DIM)
        result = attend(
            stacked, values, chunk_heads, c * chunk_heads,
            first_block, last_block, sample_ends, RESULT_DTYPE,
        )
        results.append(result)
    received = []
    for g in range(0, chunks, 2):
        group = jnp.concatenate(results[g:g + 2], axis=2)
        received.append(lax.all_to_all(
            group.reshape(2, seq_count, tokens, group.shape[2]),
            "seq", split_axis=1, concat_axis=1, tiled=True,
        ))
    results = received
    joined = jnp.concatenate(results, axis=3)
    joined = jnp.swapaxes(joined, 1, 2).reshape(2, 1, tokens, width).astype(jnp.float32)
    return (joined[0], joined[1])


def solution(mesh):
    placed = (
        P(("groups", "samp"), "seq", None),
        P(("groups", "samp"), "seq", None),
        P(("groups", "samp"), "seq", None),
        P(("groups", "samp"), "seq", None),
        P(("groups", "samp"), "seq", None),
        P(("groups", "samp"), "seq", None),
        P(),
        P(),
        P("groups", None),
    )
    return jax.shard_map(
        per_device_body,
        mesh=mesh,
        in_specs=placed,
        out_specs=(P(("groups", "samp"), "seq", None), P(("groups", "samp"), "seq", None)),
        check_vma=False,
    )
```

```python
import math

import jax
import jax.numpy as jnp
from jax import lax
from jax.experimental import pallas as pl
from jax.experimental.pallas import tpu as pltpu
from jax.sharding import PartitionSpec as P


HEAD_DIM = 128
BLOCK = 256
KEY_BLOCK = 256


def normalize(source, source_tangent, gain):
    widened = source.astype(jnp.float32)
    dwidened = source_tangent.astype(jnp.float32)
    inverse = lax.rsqrt(jnp.mean(widened * widened, axis=-1, keepdims=True) + 1e-06)
    radial = jnp.mean(widened * dwidened, axis=-1, keepdims=True)
    normed = (widened * inverse * gain).astype(jnp.bfloat16)
    tangent = ((dwidened * inverse - widened * inverse**3 * radial) * gain).astype(jnp.bfloat16)
    return (normed, tangent)


def block_tables(sample_lengths, count):
    sample_ends = jnp.cumsum(sample_lengths).astype(jnp.int32)
    sample_starts = sample_ends - sample_lengths
    blocks = count // BLOCK
    first_rows = jnp.arange(blocks, dtype=jnp.int32) * BLOCK
    last_rows = first_rows + (BLOCK - 1)
    first_segment = jnp.sum((first_rows[:, None] >= sample_ends[None, :]).astype(jnp.int32), axis=1)
    last_segment = jnp.sum((last_rows[:, None] >= sample_ends[None, :]).astype(jnp.int32), axis=1)
    samples = sample_lengths.shape[0]
    first_segment = jnp.clip(first_segment, 0, samples - 1)
    last_segment = jnp.clip(last_segment, 0, samples - 1)
    first_key = jnp.take(sample_starts, first_segment)
    last_key = jnp.take(sample_ends, last_segment)
    key_blocks = count // KEY_BLOCK
    first_block = jnp.clip(first_key // KEY_BLOCK, 0, key_blocks - 1)
    last_block = jnp.clip((last_key - 1) // KEY_BLOCK + 1, first_block + 1, key_blocks)
    return first_block.astype(jnp.int32), last_block.astype(jnp.int32), sample_ends


def attention_kernel(
    first_ref, last_ref, ends_ref,
    q_ref, dq_ref, k_ref, dk_ref, v_ref, dv_ref,
    result_ref,
):
    i = pl.program_id(1)
    samples = ends_ref.shape[0]
    factor = 1.0 / math.sqrt(HEAD_DIM)
    queries = q_ref[...]
    dqueries = dq_ref[...]
    both_queries = jnp.concatenate([dqueries, queries], axis=1)

    def segment_of(positions):
        seg = jnp.zeros(positions.shape, jnp.int32)
        for j in range(samples):
            seg = seg + (positions >= ends_ref[j]).astype(jnp.int32)
        return seg

    query_positions = i * BLOCK + lax.broadcasted_iota(jnp.int32, (BLOCK, 1), 0)
    query_segment = segment_of(query_positions)
    first = first_ref[i]
    last = last_ref[i]

    def scores_of(kb):
        start = kb * KEY_BLOCK
        key_rows = k_ref[kb]
        key_positions = start + lax.broadcasted_iota(jnp.int32, (1, KEY_BLOCK), 1)
        same = query_segment == segment_of(key_positions)
        raw = lax.dot_general(
            queries, key_rows, (((1,), (1,)), ((), ())), preferred_element_type=jnp.float32
        ) * factor
        return raw, same, start, key_rows

    def statistics(kb, carry):
        row_top, total = carry
        raw, same, _, _ = scores_of(kb)
        masked = jnp.where(same, raw, -1e30)
        new_top = jnp.maximum(row_top, jnp.max(masked, axis=1, keepdims=True))
        exponent = jnp.where(same, jnp.exp(masked - new_top), 0.0)
        total = total * jnp.exp(row_top - new_top) + jnp.sum(exponent, axis=1, keepdims=True)
        return new_top, total

    row_top, total = lax.fori_loop(
        first, last, statistics,
        (jnp.full((BLOCK, 1), -1e30, jnp.float32), jnp.zeros((BLOCK, 1), jnp.float32)),
    )
    inverse_total = 1.0 / total

    def sums(kb, carry):
        center, output, spread_sum, dvalue_sum = carry
        raw, same, _, key_rows = scores_of(kb)
        dkey_rows = dk_ref[kb]
        value_rows = v_ref[kb]
        dvalue_rows = dv_ref[kb]
        both_keys = jnp.concatenate([key_rows, dkey_rows], axis=1)
        dscores = lax.dot_general(
            both_queries, both_keys, (((1,), (1,)), ((), ())), preferred_element_type=jnp.float32
        ) * factor
        weights = jnp.where(same, jnp.exp(raw - row_top), 0.0) * inverse_total
        product = jnp.where(same, weights * dscores, 0.0)
        center = center + jnp.sum(product, axis=1, keepdims=True)
        rounded = weights.astype(jnp.bfloat16)
        spread = product.astype(jnp.bfloat16)
        output = output + jnp.dot(rounded, value_rows, preferred_element_type=jnp.float32)
        spread_sum = spread_sum + jnp.dot(spread, value_rows, preferred_element_type=jnp.float32)
        dvalue_sum = dvalue_sum + jnp.dot(rounded, dvalue_rows, preferred_element_type=jnp.float32)
        return center, output, spread_sum, dvalue_sum

    empty = jnp.zeros((BLOCK, HEAD_DIM), jnp.float32)
    center, output, spread_sum, dvalue_sum = lax.fori_loop(
        first, last, sums, (jnp.zeros((BLOCK, 1), jnp.float32), empty, empty, empty)
    )
    result_ref[0] = output.astype(result_ref.dtype)
    result_ref[1] = (spread_sum - center * output + dvalue_sum).astype(result_ref.dtype)


def attend(stacked, values, heads, offset, first_block, last_block, sample_ends, result_dtype):
    sources = stacked.shape[0]
    all_heads = values.shape[1] // 2

    def query_spec(t):
        return pl.BlockSpec((None, None, BLOCK, HEAD_DIM), lambda h, i, *_: (i, t * heads + h, 0, 0))

    def key_spec(t):
        return pl.BlockSpec((sources, None, BLOCK, HEAD_DIM), lambda h, i, *_: (0, t * heads + h, 0, 0))

    def value_spec(t):
        return pl.BlockSpec(
            (sources, None, BLOCK, HEAD_DIM), lambda h, i, *_: (0, t * all_heads + offset + h, 0, 0)
        )

    grid_spec = pltpu.PrefetchScalarGridSpec(
        num_scalar_prefetch=3,
        grid=(heads, sources),
        in_specs=[query_spec(0), query_spec(1), key_spec(2), key_spec(3), value_spec(0), value_spec(1)],
        out_specs=pl.BlockSpec((None, 2, BLOCK, HEAD_DIM), lambda h, i, *_: (i, 0, 0, h)),
    )
    return pl.pallas_call(
        attention_kernel,
        grid_spec=grid_spec,
        out_shape=jax.ShapeDtypeStruct((sources, 2, BLOCK, heads * HEAD_DIM), result_dtype),
        compiler_params=pltpu.CompilerParams(
            dimension_semantics=("arbitrary", "arbitrary"),
        ),
    )(first_block, last_block, sample_ends, stacked, stacked, stacked, stacked, values, values)


def assemble_kernel(*refs):
    *received, out_ref, tan_ref = refs
    offset = 0
    for r in received:
        w = r.shape[-1]
        out_ref[:, offset:offset + w] = r[0].astype(jnp.float32)
        tan_ref[:, offset:offset + w] = r[1].astype(jnp.float32)
        offset += w


def assemble(received, tokens, width):
    sources = received[0].shape[0]
    local_width = width // sources
    in_specs = [
        pl.BlockSpec((None, 2, tokens, r.shape[3]), lambda s: (s, 0, 0, 0)) for r in received
    ]
    out_spec = pl.BlockSpec((None, tokens, local_width), lambda s: (0, 0, s))
    return pl.pallas_call(
        assemble_kernel,
        grid=(sources,),
        in_specs=in_specs,
        out_specs=[out_spec, out_spec],
        out_shape=[
            jax.ShapeDtypeStruct((1, tokens, width), jnp.float32),
            jax.ShapeDtypeStruct((1, tokens, width), jnp.float32),
        ],
    )(*received)


CHUNKS = 4
RESULT_DTYPE = jnp.bfloat16


def per_device_body(
    q_proj, q_tangent, k_proj, k_tangent, v_proj, v_tangent, query_norm_gain, key_norm_gain, lengths
):
    seq_count = lax.axis_size("seq")
    tokens = q_proj.shape[1]
    width = q_proj.shape[2]
    local_heads = width // HEAD_DIM // seq_count
    pack_tokens = tokens * seq_count
    chunks = min(CHUNKS, local_heads)
    chunk_heads = local_heads // chunks

    assert tokens == BLOCK

    def by_destination(array, heads):
        split = array.reshape(tokens, seq_count, local_heads, HEAD_DIM)[:, :, heads]
        return jnp.transpose(split, (1, 2, 0, 3))

    value_payload = jnp.concatenate(
        [by_destination(array, slice(0, local_heads)) for array in (v_proj, v_tangent)], axis=1
    )
    values = lax.all_to_all(value_payload, "seq", split_axis=0, concat_axis=0, tiled=True)

    q_normed, dq_normed = normalize(q_proj, q_tangent, query_norm_gain)
    k_normed, dk_normed = normalize(k_proj, k_tangent, key_norm_gain)
    own_row = lax.dynamic_slice_in_dim(lengths, lax.axis_index("samp"), 1, 0)[0]
    first_block, last_block, sample_ends = block_tables(own_row, pack_tokens)
    normed = (q_normed, dq_normed, k_normed, dk_normed)
    results = []
    for c in range(chunks):
        heads = slice(c * chunk_heads, (c + 1) * chunk_heads)
        payload = jnp.concatenate([by_destination(array, heads) for array in normed], axis=1)
        stacked = lax.all_to_all(payload, "seq", split_axis=0, concat_axis=0, tiled=True)
        result = attend(
            stacked, values, chunk_heads, c * chunk_heads,
            first_block, last_block, sample_ends, RESULT_DTYPE,
        )
        results.append(result)
    received = []
    for g in range(0, chunks, 2):
        group = jnp.concatenate(results[g:g + 2], axis=3)
        received.append(lax.all_to_all(group, "seq", split_axis=0, concat_axis=0, tiled=True))
    return tuple(assemble(received, tokens, width))


def solution(mesh):
    placed = (
        P(("groups", "samp"), "seq", None),
        P(("groups", "samp"), "seq", None),
        P(("groups", "samp"), "seq", None),
        P(("groups", "samp"), "seq", None),
        P(("groups", "samp"), "seq", None),
        P(("groups", "samp"), "seq", None),
        P(),
        P(),
        P("groups", None),
    )
    return jax.shard_map(
        per_device_body,
        mesh=mesh,
        in_specs=placed,
        out_specs=(P(("groups", "samp"), "seq", None), P(("groups", "samp"), "seq", None)),
        check_vma=False,
    )
```

```python
import math

import jax
import jax.numpy as jnp
from jax import lax
from jax.experimental import pallas as pl
from jax.experimental.pallas import tpu as pltpu
from jax.sharding import PartitionSpec as P


HEAD_DIM = 128
BLOCK = 256
KEY_BLOCK = 256


def normalize(source, source_tangent, gain):
    widened = source.astype(jnp.float32)
    dwidened = source_tangent.astype(jnp.float32)
    inverse = lax.rsqrt(jnp.mean(widened * widened, axis=-1, keepdims=True) + 1e-06)
    radial = jnp.mean(widened * dwidened, axis=-1, keepdims=True)
    normed = (widened * inverse * gain).astype(jnp.bfloat16)
    tangent = ((dwidened * inverse - widened * inverse**3 * radial) * gain).astype(jnp.bfloat16)
    return (normed, tangent)


def block_tables(sample_lengths, count):
    sample_ends = jnp.cumsum(sample_lengths).astype(jnp.int32)
    sample_starts = sample_ends - sample_lengths
    blocks = count // BLOCK
    first_rows = jnp.arange(blocks, dtype=jnp.int32) * BLOCK
    last_rows = first_rows + (BLOCK - 1)
    first_segment = jnp.sum((first_rows[:, None] >= sample_ends[None, :]).astype(jnp.int32), axis=1)
    last_segment = jnp.sum((last_rows[:, None] >= sample_ends[None, :]).astype(jnp.int32), axis=1)
    samples = sample_lengths.shape[0]
    first_segment = jnp.clip(first_segment, 0, samples - 1)
    last_segment = jnp.clip(last_segment, 0, samples - 1)
    first_key = jnp.take(sample_starts, first_segment)
    last_key = jnp.take(sample_ends, last_segment)
    key_blocks = count // KEY_BLOCK
    first_block = jnp.clip(first_key // KEY_BLOCK, 0, key_blocks - 1)
    last_block = jnp.clip((last_key - 1) // KEY_BLOCK + 1, first_block + 1, key_blocks)
    return first_block.astype(jnp.int32), last_block.astype(jnp.int32), sample_ends


def attention_kernel(
    first_ref, last_ref, ends_ref,
    q_ref, dq_ref, k_ref, dk_ref, v_ref, dv_ref,
    result_ref,
):
    i = pl.program_id(1)
    samples = ends_ref.shape[0]
    factor = 1.0 / math.sqrt(HEAD_DIM)
    queries = q_ref[...]
    dqueries = dq_ref[...]
    both_queries = jnp.concatenate([dqueries, queries], axis=1)

    def segment_of(positions):
        seg = jnp.zeros(positions.shape, jnp.int32)
        for j in range(samples):
            seg = seg + (positions >= ends_ref[j]).astype(jnp.int32)
        return seg

    query_positions = i * BLOCK + lax.broadcasted_iota(jnp.int32, (BLOCK, 1), 0)
    query_segment = segment_of(query_positions)
    first = first_ref[i]
    last = last_ref[i]

    def scores_of(kb):
        start = kb * KEY_BLOCK
        key_rows = k_ref[kb]
        key_positions = start + lax.broadcasted_iota(jnp.int32, (1, KEY_BLOCK), 1)
        same = query_segment == segment_of(key_positions)
        raw = lax.dot_general(
            queries, key_rows, (((1,), (1,)), ((), ())), preferred_element_type=jnp.float32
        ) * factor
        return raw, same, start, key_rows

    def statistics(kb, carry):
        row_top, total = carry
        raw, same, _, _ = scores_of(kb)
        masked = jnp.where(same, raw, -1e30)
        new_top = jnp.maximum(row_top, jnp.max(masked, axis=1, keepdims=True))
        exponent = jnp.where(same, jnp.exp(masked - new_top), 0.0)
        total = total * jnp.exp(row_top - new_top) + jnp.sum(exponent, axis=1, keepdims=True)
        return new_top, total

    row_top, total = lax.fori_loop(
        first, last, statistics,
        (jnp.full((BLOCK, 1), -1e30, jnp.float32), jnp.zeros((BLOCK, 1), jnp.float32)),
    )
    inverse_total = 1.0 / total

    def sums(kb, carry):
        center, output, spread_sum, dvalue_sum = carry
        raw, same, _, key_rows = scores_of(kb)
        dkey_rows = dk_ref[kb]
        value_rows = v_ref[kb]
        dvalue_rows = dv_ref[kb]
        both_keys = jnp.concatenate([key_rows, dkey_rows], axis=1)
        dscores = lax.dot_general(
            both_queries, both_keys, (((1,), (1,)), ((), ())), preferred_element_type=jnp.float32
        ) * factor
        weights = jnp.where(same, jnp.exp(raw - row_top), 0.0) * inverse_total
        product = jnp.where(same, weights * dscores, 0.0)
        center = center + jnp.sum(product, axis=1, keepdims=True)
        rounded = weights.astype(jnp.bfloat16)
        spread = product.astype(jnp.bfloat16)
        output = output + jnp.dot(rounded, value_rows, preferred_element_type=jnp.float32)
        spread_sum = spread_sum + jnp.dot(spread, value_rows, preferred_element_type=jnp.float32)
        dvalue_sum = dvalue_sum + jnp.dot(rounded, dvalue_rows, preferred_element_type=jnp.float32)
        return center, output, spread_sum, dvalue_sum

    empty = jnp.zeros((BLOCK, HEAD_DIM), jnp.float32)
    center, output, spread_sum, dvalue_sum = lax.fori_loop(
        first, last, sums, (jnp.zeros((BLOCK, 1), jnp.float32), empty, empty, empty)
    )
    result_ref[0] = output.astype(result_ref.dtype)
    result_ref[1] = (spread_sum - center * output + dvalue_sum).astype(result_ref.dtype)


def attend(stacked, values, heads, offset, first_block, last_block, sample_ends, result_dtype):
    sources = stacked.shape[0]
    all_heads = values.shape[1] // 2

    def query_spec(t):
        return pl.BlockSpec((None, None, BLOCK, HEAD_DIM), lambda h, i, *_: (i, t * heads + h, 0, 0))

    def key_spec(t):
        return pl.BlockSpec((sources, None, BLOCK, HEAD_DIM), lambda h, i, *_: (0, t * heads + h, 0, 0))

    def value_spec(t):
        return pl.BlockSpec(
            (sources, None, BLOCK, HEAD_DIM), lambda h, i, *_: (0, t * all_heads + offset + h, 0, 0)
        )

    grid_spec = pltpu.PrefetchScalarGridSpec(
        num_scalar_prefetch=3,
        grid=(heads, sources),
        in_specs=[query_spec(0), query_spec(1), key_spec(2), key_spec(3), value_spec(0), value_spec(1)],
        out_specs=pl.BlockSpec((None, 2, BLOCK, HEAD_DIM), lambda h, i, *_: (i, 0, 0, h)),
    )
    return pl.pallas_call(
        attention_kernel,
        grid_spec=grid_spec,
        out_shape=jax.ShapeDtypeStruct((sources, 2, BLOCK, heads * HEAD_DIM), result_dtype),
        compiler_params=pltpu.CompilerParams(
            dimension_semantics=("arbitrary", "arbitrary"),
        ),
    )(first_block, last_block, sample_ends, stacked, stacked, stacked, stacked, values, values)


def gather_kernel(*refs):
    *sources, out_ref = refs
    heads = out_ref.shape[0] // len(sources)
    for t, ref in enumerate(sources):
        for h in range(heads):
            out_ref[t * heads + h] = ref[:, h * HEAD_DIM:(h + 1) * HEAD_DIM]


def by_destination_all(arrays, destinations):
    tokens, width = arrays[0].shape[1], arrays[0].shape[2]
    local_width = width // destinations
    heads = local_width // HEAD_DIM
    in_spec = pl.BlockSpec((None, tokens, local_width), lambda d: (0, 0, d))
    return pl.pallas_call(
        gather_kernel,
        grid=(destinations,),
        in_specs=[in_spec] * len(arrays),
        out_specs=pl.BlockSpec((None, len(arrays) * heads, tokens, HEAD_DIM), lambda d: (d, 0, 0, 0)),
        out_shape=jax.ShapeDtypeStruct(
            (destinations, len(arrays) * heads, tokens, HEAD_DIM), arrays[0].dtype
        ),
    )(*arrays)


def assemble_kernel(*refs):
    *received, out_ref, tan_ref = refs
    offset = 0
    for r in received:
        w = r.shape[-1]
        out_ref[:, offset:offset + w] = r[0].astype(jnp.float32)
        tan_ref[:, offset:offset + w] = r[1].astype(jnp.float32)
        offset += w


def assemble(received, tokens, width):
    sources = received[0].shape[0]
    local_width = width // sources
    in_specs = [
        pl.BlockSpec((None, 2, tokens, r.shape[3]), lambda s: (s, 0, 0, 0)) for r in received
    ]
    out_spec = pl.BlockSpec((None, tokens, local_width), lambda s: (0, 0, s))
    return pl.pallas_call(
        assemble_kernel,
        grid=(sources,),
        in_specs=in_specs,
        out_specs=[out_spec, out_spec],
        out_shape=[
            jax.ShapeDtypeStruct((1, tokens, width), jnp.float32),
            jax.ShapeDtypeStruct((1, tokens, width), jnp.float32),
        ],
    )(*received)


CHUNKS = 4
RESULT_DTYPE = jnp.bfloat16


def per_device_body(
    q_proj, q_tangent, k_proj, k_tangent, v_proj, v_tangent, query_norm_gain, key_norm_gain, lengths
):
    seq_count = lax.axis_size("seq")
    tokens = q_proj.shape[1]
    width = q_proj.shape[2]
    local_heads = width // HEAD_DIM // seq_count
    pack_tokens = tokens * seq_count
    chunks = min(CHUNKS, local_heads)
    chunk_heads = local_heads // chunks

    assert tokens == BLOCK

    def by_destination(array, heads):
        split = array.reshape(tokens, seq_count, local_heads, HEAD_DIM)[:, :, heads]
        return jnp.transpose(split, (1, 2, 0, 3))

    value_payload = by_destination_all((v_proj, v_tangent), seq_count)
    values = lax.all_to_all(value_payload, "seq", split_axis=0, concat_axis=0, tiled=True)

    q_normed, dq_normed = normalize(q_proj, q_tangent, query_norm_gain)
    k_normed, dk_normed = normalize(k_proj, k_tangent, key_norm_gain)
    own_row = lax.dynamic_slice_in_dim(lengths, lax.axis_index("samp"), 1, 0)[0]
    first_block, last_block, sample_ends = block_tables(own_row, pack_tokens)
    normed = (q_normed, dq_normed, k_normed, dk_normed)
    results = []
    for c in range(chunks):
        heads = slice(c * chunk_heads, (c + 1) * chunk_heads)
        payload = jnp.concatenate([by_destination(array, heads) for array in normed], axis=1)
        stacked = lax.all_to_all(payload, "seq", split_axis=0, concat_axis=0, tiled=True)
        result = attend(
            stacked, values, chunk_heads, c * chunk_heads,
            first_block, last_block, sample_ends, RESULT_DTYPE,
        )
        results.append(result)
    received = []
    for g in range(0, chunks, 2):
        group = jnp.concatenate(results[g:g + 2], axis=3)
        received.append(lax.all_to_all(group, "seq", split_axis=0, concat_axis=0, tiled=True))
    return tuple(assemble(received, tokens, width))


def solution(mesh):
    placed = (
        P(("groups", "samp"), "seq", None),
        P(("groups", "samp"), "seq", None),
        P(("groups", "samp"), "seq", None),
        P(("groups", "samp"), "seq", None),
        P(("groups", "samp"), "seq", None),
        P(("groups", "samp"), "seq", None),
        P(),
        P(),
        P("groups", None),
    )
    return jax.shard_map(
        per_device_body,
        mesh=mesh,
        in_specs=placed,
        out_specs=(P(("groups", "samp"), "seq", None), P(("groups", "samp"), "seq", None)),
        check_vma=False,
    )
```

```python
import math

import jax
import jax.numpy as jnp
from jax import lax
from jax.experimental import pallas as pl
from jax.experimental.pallas import tpu as pltpu
from jax.sharding import PartitionSpec as P


HEAD_DIM = 128
BLOCK = 256
KEY_BLOCK = 256


def normalize(source, source_tangent, gain):
    widened = source.astype(jnp.float32)
    dwidened = source_tangent.astype(jnp.float32)
    inverse = lax.rsqrt(jnp.mean(widened * widened, axis=-1, keepdims=True) + 1e-06)
    radial = jnp.mean(widened * dwidened, axis=-1, keepdims=True)
    normed = (widened * inverse * gain).astype(jnp.bfloat16)
    tangent = ((dwidened * inverse - widened * inverse**3 * radial) * gain).astype(jnp.bfloat16)
    return (normed, tangent)


def block_tables(sample_lengths, count):
    sample_ends = jnp.cumsum(sample_lengths).astype(jnp.int32)
    sample_starts = sample_ends - sample_lengths
    blocks = count // BLOCK
    first_rows = jnp.arange(blocks, dtype=jnp.int32) * BLOCK
    last_rows = first_rows + (BLOCK - 1)
    first_segment = jnp.sum((first_rows[:, None] >= sample_ends[None, :]).astype(jnp.int32), axis=1)
    last_segment = jnp.sum((last_rows[:, None] >= sample_ends[None, :]).astype(jnp.int32), axis=1)
    samples = sample_lengths.shape[0]
    first_segment = jnp.clip(first_segment, 0, samples - 1)
    last_segment = jnp.clip(last_segment, 0, samples - 1)
    first_key = jnp.take(sample_starts, first_segment)
    last_key = jnp.take(sample_ends, last_segment)
    key_blocks = count // KEY_BLOCK
    first_block = jnp.clip(first_key // KEY_BLOCK, 0, key_blocks - 1)
    last_block = jnp.clip((last_key - 1) // KEY_BLOCK + 1, first_block + 1, key_blocks)
    return first_block.astype(jnp.int32), last_block.astype(jnp.int32), sample_ends


def attention_kernel(
    first_ref, last_ref, ends_ref,
    q_ref, dq_ref, k_ref, dk_ref, v_ref, dv_ref,
    result_ref,
):
    i = pl.program_id(1)
    samples = ends_ref.shape[0]
    factor = 1.0 / math.sqrt(HEAD_DIM)
    queries = q_ref[...]
    dqueries = dq_ref[...]
    both_queries = jnp.concatenate([dqueries, queries], axis=1)

    def segment_of(positions):
        seg = jnp.zeros(positions.shape, jnp.int32)
        for j in range(samples):
            seg = seg + (positions >= ends_ref[j]).astype(jnp.int32)
        return seg

    query_positions = i * BLOCK + lax.broadcasted_iota(jnp.int32, (BLOCK, 1), 0)
    query_segment = segment_of(query_positions)
    first = first_ref[i]
    last = last_ref[i]

    def scores_of(kb):
        start = kb * KEY_BLOCK
        key_rows = k_ref[kb]
        key_positions = start + lax.broadcasted_iota(jnp.int32, (1, KEY_BLOCK), 1)
        same = query_segment == segment_of(key_positions)
        raw = lax.dot_general(
            queries, key_rows, (((1,), (1,)), ((), ())), preferred_element_type=jnp.float32
        ) * factor
        return raw, same, start, key_rows

    def statistics(kb, carry):
        row_top, total = carry
        raw, same, _, _ = scores_of(kb)
        masked = jnp.where(same, raw, -1e30)
        new_top = jnp.maximum(row_top, jnp.max(masked, axis=1, keepdims=True))
        exponent = jnp.where(same, jnp.exp(masked - new_top), 0.0)
        total = total * jnp.exp(row_top - new_top) + jnp.sum(exponent, axis=1, keepdims=True)
        return new_top, total

    row_top, total = lax.fori_loop(
        first, last, statistics,
        (jnp.full((BLOCK, 1), -1e30, jnp.float32), jnp.zeros((BLOCK, 1), jnp.float32)),
    )
    inverse_total = 1.0 / total

    def sums(kb, carry):
        center, output, spread_sum, dvalue_sum = carry
        raw, same, _, key_rows = scores_of(kb)
        dkey_rows = dk_ref[kb]
        value_rows = v_ref[kb]
        dvalue_rows = dv_ref[kb]
        both_keys = jnp.concatenate([key_rows, dkey_rows], axis=1)
        dscores = lax.dot_general(
            both_queries, both_keys, (((1,), (1,)), ((), ())), preferred_element_type=jnp.float32
        ) * factor
        weights = jnp.where(same, jnp.exp(raw - row_top), 0.0) * inverse_total
        product = jnp.where(same, weights * dscores, 0.0)
        center = center + jnp.sum(product, axis=1, keepdims=True)
        rounded = weights.astype(jnp.bfloat16)
        spread = product.astype(jnp.bfloat16)
        output = output + jnp.dot(rounded, value_rows, preferred_element_type=jnp.float32)
        spread_sum = spread_sum + jnp.dot(spread, value_rows, preferred_element_type=jnp.float32)
        dvalue_sum = dvalue_sum + jnp.dot(rounded, dvalue_rows, preferred_element_type=jnp.float32)
        return center, output, spread_sum, dvalue_sum

    empty = jnp.zeros((BLOCK, HEAD_DIM), jnp.float32)
    center, output, spread_sum, dvalue_sum = lax.fori_loop(
        first, last, sums, (jnp.zeros((BLOCK, 1), jnp.float32), empty, empty, empty)
    )
    result_ref[0] = output.astype(result_ref.dtype)
    result_ref[1] = (spread_sum - center * output + dvalue_sum).astype(result_ref.dtype)


def attend(stacked, values, heads, offset, first_block, last_block, sample_ends, result_dtype):
    sources = stacked.shape[0]
    all_heads = values.shape[1] // 2

    def query_spec(t):
        return pl.BlockSpec((None, None, BLOCK, HEAD_DIM), lambda h, i, *_: (i, t * heads + h, 0, 0))

    def key_spec(t):
        return pl.BlockSpec((sources, None, BLOCK, HEAD_DIM), lambda h, i, *_: (0, t * heads + h, 0, 0))

    def value_spec(t):
        return pl.BlockSpec(
            (sources, None, BLOCK, HEAD_DIM), lambda h, i, *_: (0, t * all_heads + offset + h, 0, 0)
        )

    grid_spec = pltpu.PrefetchScalarGridSpec(
        num_scalar_prefetch=3,
        grid=(heads, sources),
        in_specs=[query_spec(0), query_spec(1), key_spec(2), key_spec(3), value_spec(0), value_spec(1)],
        out_specs=pl.BlockSpec((None, 2, BLOCK, HEAD_DIM), lambda h, i, *_: (i, 0, 0, h)),
    )
    return pl.pallas_call(
        attention_kernel,
        grid_spec=grid_spec,
        out_shape=jax.ShapeDtypeStruct((sources, 2, BLOCK, heads * HEAD_DIM), result_dtype),
        compiler_params=pltpu.CompilerParams(
            dimension_semantics=("arbitrary", "arbitrary"),
        ),
    )(first_block, last_block, sample_ends, stacked, stacked, stacked, stacked, values, values)


def gather_kernel(*refs):
    *sources, out_ref = refs
    heads = out_ref.shape[0] // len(sources)
    for t, ref in enumerate(sources):
        for h in range(heads):
            out_ref[t * heads + h] = ref[:, h * HEAD_DIM:(h + 1) * HEAD_DIM]


def by_destination_all(arrays, destinations):
    tokens, width = arrays[0].shape[1], arrays[0].shape[2]
    local_width = width // destinations
    heads = local_width // HEAD_DIM
    in_spec = pl.BlockSpec((None, tokens, local_width), lambda d: (0, 0, d))
    return pl.pallas_call(
        gather_kernel,
        grid=(destinations,),
        in_specs=[in_spec] * len(arrays),
        out_specs=pl.BlockSpec((None, len(arrays) * heads, tokens, HEAD_DIM), lambda d: (d, 0, 0, 0)),
        out_shape=jax.ShapeDtypeStruct(
            (destinations, len(arrays) * heads, tokens, HEAD_DIM), arrays[0].dtype
        ),
    )(*arrays)


def assemble_kernel(received_ref, *refs):
    out_ref, tan_ref = refs[-2], refs[-1]
    out_ref[...] = received_ref[0].astype(jnp.float32)
    tan_ref[...] = received_ref[1].astype(jnp.float32)


def assemble_part(received, part, parts, previous, tokens, width):
    sources, _, _, part_width = received.shape
    in_specs = [pl.BlockSpec((None, 2, tokens, part_width), lambda s: (s, 0, 0, 0))]
    out_spec = pl.BlockSpec((None, tokens, part_width), lambda s: (0, 0, s * parts + part))
    operands = [received]
    aliases = {}
    if previous is not None:
        in_specs += [pl.BlockSpec(memory_space=pl.ANY), pl.BlockSpec(memory_space=pl.ANY)]
        operands += list(previous)
        aliases = {1: 0, 2: 1}
    return pl.pallas_call(
        assemble_kernel,
        grid=(sources,),
        in_specs=in_specs,
        out_specs=[out_spec, out_spec],
        out_shape=[
            jax.ShapeDtypeStruct((1, tokens, width), jnp.float32),
            jax.ShapeDtypeStruct((1, tokens, width), jnp.float32),
        ],
        input_output_aliases=aliases,
    )(*operands)


CHUNKS = 4
RESULT_DTYPE = jnp.bfloat16


def per_device_body(
    q_proj, q_tangent, k_proj, k_tangent, v_proj, v_tangent, query_norm_gain, key_norm_gain, lengths
):
    seq_count = lax.axis_size("seq")
    tokens = q_proj.shape[1]
    width = q_proj.shape[2]
    local_heads = width // HEAD_DIM // seq_count
    pack_tokens = tokens * seq_count
    chunks = min(CHUNKS, local_heads)
    chunk_heads = local_heads // chunks

    assert tokens == BLOCK

    def by_destination(array, heads):
        split = array.reshape(tokens, seq_count, local_heads, HEAD_DIM)[:, :, heads]
        return jnp.transpose(split, (1, 2, 0, 3))

    value_payload = by_destination_all((v_proj, v_tangent), seq_count)
    values = lax.all_to_all(value_payload, "seq", split_axis=0, concat_axis=0, tiled=True)

    q_normed, dq_normed = normalize(q_proj, q_tangent, query_norm_gain)
    k_normed, dk_normed = normalize(k_proj, k_tangent, key_norm_gain)
    own_row = lax.dynamic_slice_in_dim(lengths, lax.axis_index("samp"), 1, 0)[0]
    first_block, last_block, sample_ends = block_tables(own_row, pack_tokens)
    normed = (q_normed, dq_normed, k_normed, dk_normed)
    results = []
    for c in range(chunks):
        heads = slice(c * chunk_heads, (c + 1) * chunk_heads)
        payload = jnp.concatenate([by_destination(array, heads) for array in normed], axis=1)
        stacked = lax.all_to_all(payload, "seq", split_axis=0, concat_axis=0, tiled=True)
        result = attend(
            stacked, values, chunk_heads, c * chunk_heads,
            first_block, last_block, sample_ends, RESULT_DTYPE,
        )
        results.append(result)
    groups = [results[g:g + 2] for g in range(0, chunks, 2)]
    outputs = None
    for g, members in enumerate(groups):
        group = jnp.concatenate(members, axis=3)
        received = lax.all_to_all(group, "seq", split_axis=0, concat_axis=0, tiled=True)
        outputs = assemble_part(received, g, len(groups), outputs, tokens, width)
    return tuple(outputs)


def solution(mesh):
    placed = (
        P(("groups", "samp"), "seq", None),
        P(("groups", "samp"), "seq", None),
        P(("groups", "samp"), "seq", None),
        P(("groups", "samp"), "seq", None),
        P(("groups", "samp"), "seq", None),
        P(("groups", "samp"), "seq", None),
        P(),
        P(),
        P("groups", None),
    )
    return jax.shard_map(
        per_device_body,
        mesh=mesh,
        in_specs=placed,
        out_specs=(P(("groups", "samp"), "seq", None), P(("groups", "samp"), "seq", None)),
        check_vma=False,
    )
```

```python
import math

import jax
import jax.numpy as jnp
from jax import lax
from jax.experimental import pallas as pl
from jax.experimental.pallas import tpu as pltpu
from jax.sharding import PartitionSpec as P


HEAD_DIM = 128
BLOCK = 256
KEY_BLOCK = 256


def normalize(source, source_tangent, gain):
    widened = source.astype(jnp.float32)
    dwidened = source_tangent.astype(jnp.float32)
    inverse = lax.rsqrt(jnp.mean(widened * widened, axis=-1, keepdims=True) + 1e-06)
    radial = jnp.mean(widened * dwidened, axis=-1, keepdims=True)
    normed = (widened * inverse * gain).astype(jnp.bfloat16)
    tangent = ((dwidened * inverse - widened * inverse**3 * radial) * gain).astype(jnp.bfloat16)
    return (normed, tangent)


def block_tables(sample_lengths, count):
    sample_ends = jnp.cumsum(sample_lengths).astype(jnp.int32)
    sample_starts = sample_ends - sample_lengths
    blocks = count // BLOCK
    first_rows = jnp.arange(blocks, dtype=jnp.int32) * BLOCK
    last_rows = first_rows + (BLOCK - 1)
    first_segment = jnp.sum((first_rows[:, None] >= sample_ends[None, :]).astype(jnp.int32), axis=1)
    last_segment = jnp.sum((last_rows[:, None] >= sample_ends[None, :]).astype(jnp.int32), axis=1)
    samples = sample_lengths.shape[0]
    first_segment = jnp.clip(first_segment, 0, samples - 1)
    last_segment = jnp.clip(last_segment, 0, samples - 1)
    first_key = jnp.take(sample_starts, first_segment)
    last_key = jnp.take(sample_ends, last_segment)
    key_blocks = count // KEY_BLOCK
    first_block = jnp.clip(first_key // KEY_BLOCK, 0, key_blocks - 1)
    last_block = jnp.clip((last_key - 1) // KEY_BLOCK + 1, first_block + 1, key_blocks)
    return first_block.astype(jnp.int32), last_block.astype(jnp.int32), sample_ends


def attention_kernel(
    first_ref, last_ref, ends_ref,
    q_ref, dq_ref, k_ref, dk_ref, v_ref, dv_ref,
    result_ref,
):
    i = pl.program_id(1)
    samples = ends_ref.shape[0]
    factor = 1.0 / math.sqrt(HEAD_DIM)
    queries = q_ref[...]
    dqueries = dq_ref[...]
    both_queries = jnp.concatenate([dqueries, queries], axis=1)

    def segment_of(positions):
        seg = jnp.zeros(positions.shape, jnp.int32)
        for j in range(samples):
            seg = seg + (positions >= ends_ref[j]).astype(jnp.int32)
        return seg

    query_positions = i * BLOCK + lax.broadcasted_iota(jnp.int32, (BLOCK, 1), 0)
    query_segment = segment_of(query_positions)
    first = first_ref[i]
    last = last_ref[i]

    def scores_of(kb):
        start = kb * KEY_BLOCK
        key_rows = k_ref[kb]
        key_positions = start + lax.broadcasted_iota(jnp.int32, (1, KEY_BLOCK), 1)
        same = query_segment == segment_of(key_positions)
        raw = lax.dot_general(
            queries, key_rows, (((1,), (1,)), ((), ())), preferred_element_type=jnp.float32
        ) * factor
        return raw, same, start, key_rows

    def statistics(kb, carry):
        row_top, total = carry
        raw, same, _, _ = scores_of(kb)
        masked = jnp.where(same, raw, -1e30)
        new_top = jnp.maximum(row_top, jnp.max(masked, axis=1, keepdims=True))
        exponent = jnp.where(same, jnp.exp(masked - new_top), 0.0)
        total = total * jnp.exp(row_top - new_top) + jnp.sum(exponent, axis=1, keepdims=True)
        return new_top, total

    row_top, total = lax.fori_loop(
        first, last, statistics,
        (jnp.full((BLOCK, 1), -1e30, jnp.float32), jnp.zeros((BLOCK, 1), jnp.float32)),
    )
    inverse_total = 1.0 / total

    def sums(kb, carry):
        center, output, spread_sum, dvalue_sum = carry
        raw, same, _, key_rows = scores_of(kb)
        dkey_rows = dk_ref[kb]
        value_rows = v_ref[kb]
        dvalue_rows = dv_ref[kb]
        both_keys = jnp.concatenate([key_rows, dkey_rows], axis=1)
        dscores = lax.dot_general(
            both_queries, both_keys, (((1,), (1,)), ((), ())), preferred_element_type=jnp.float32
        ) * factor
        weights = jnp.where(same, jnp.exp(raw - row_top), 0.0) * inverse_total
        product = jnp.where(same, weights * dscores, 0.0)
        center = center + jnp.sum(product, axis=1, keepdims=True)
        rounded = weights.astype(jnp.bfloat16)
        spread = product.astype(jnp.bfloat16)
        output = output + jnp.dot(rounded, value_rows, preferred_element_type=jnp.float32)
        spread_sum = spread_sum + jnp.dot(spread, value_rows, preferred_element_type=jnp.float32)
        dvalue_sum = dvalue_sum + jnp.dot(rounded, dvalue_rows, preferred_element_type=jnp.float32)
        return center, output, spread_sum, dvalue_sum

    empty = jnp.zeros((BLOCK, HEAD_DIM), jnp.float32)
    center, output, spread_sum, dvalue_sum = lax.fori_loop(
        first, last, sums, (jnp.zeros((BLOCK, 1), jnp.float32), empty, empty, empty)
    )
    result_ref[0] = output.astype(result_ref.dtype)
    result_ref[1] = (spread_sum - center * output + dvalue_sum).astype(result_ref.dtype)


def attend(stacked, values, heads, offset, first_block, last_block, sample_ends, result_dtype):
    sources = stacked.shape[0]
    all_heads = values.shape[1] // 2

    def query_spec(t):
        return pl.BlockSpec((None, None, BLOCK, HEAD_DIM), lambda h, i, *_: (i, t * heads + h, 0, 0))

    def key_spec(t):
        return pl.BlockSpec((sources, None, BLOCK, HEAD_DIM), lambda h, i, *_: (0, t * heads + h, 0, 0))

    def value_spec(t):
        return pl.BlockSpec(
            (sources, None, BLOCK, HEAD_DIM), lambda h, i, *_: (0, t * all_heads + offset + h, 0, 0)
        )

    grid_spec = pltpu.PrefetchScalarGridSpec(
        num_scalar_prefetch=3,
        grid=(heads, sources),
        in_specs=[query_spec(0), query_spec(1), key_spec(2), key_spec(3), value_spec(0), value_spec(1)],
        out_specs=pl.BlockSpec((None, 2, BLOCK, HEAD_DIM), lambda h, i, *_: (i, 0, 0, h)),
    )
    return pl.pallas_call(
        attention_kernel,
        grid_spec=grid_spec,
        out_shape=jax.ShapeDtypeStruct((sources, 2, BLOCK, heads * HEAD_DIM), result_dtype),
        compiler_params=pltpu.CompilerParams(
            dimension_semantics=("arbitrary", "arbitrary"),
        ),
    )(first_block, last_block, sample_ends, stacked, stacked, stacked, stacked, values, values)


def gather_kernel(*refs):
    *sources, out_ref = refs
    per_step = out_ref.shape[0]
    heads = out_ref.shape[1] // len(sources)
    for d in range(per_step):
        for t, ref in enumerate(sources):
            for h in range(heads):
                column = (d * heads + h) * HEAD_DIM
                out_ref[d, t * heads + h] = ref[:, column:column + HEAD_DIM]


GATHER_STEPS = 2


def by_destination_all(arrays, destinations):
    tokens, width = arrays[0].shape[1], arrays[0].shape[2]
    local_width = width // destinations
    heads = local_width // HEAD_DIM
    steps = GATHER_STEPS if destinations % GATHER_STEPS == 0 else 1
    per_step = destinations // steps
    in_spec = pl.BlockSpec((None, tokens, per_step * local_width), lambda d: (0, 0, d))
    return pl.pallas_call(
        gather_kernel,
        grid=(steps,),
        in_specs=[in_spec] * len(arrays),
        out_specs=pl.BlockSpec(
            (per_step, len(arrays) * heads, tokens, HEAD_DIM), lambda d: (d, 0, 0, 0)
        ),
        out_shape=jax.ShapeDtypeStruct(
            (destinations, len(arrays) * heads, tokens, HEAD_DIM), arrays[0].dtype
        ),
    )(*arrays)


def assemble_kernel(*refs):
    *received, out_ref, tan_ref = refs
    per_step = received[0].shape[0]
    local_width = out_ref.shape[1] // per_step
    for s in range(per_step):
        offset = s * local_width
        for r in received:
            w = r.shape[-1]
            out_ref[:, offset:offset + w] = r[s, 0].astype(jnp.float32)
            tan_ref[:, offset:offset + w] = r[s, 1].astype(jnp.float32)
            offset += w


ASSEMBLE_STEPS = 2


def assemble(received, tokens, width):
    sources = received[0].shape[0]
    local_width = width // sources
    steps = ASSEMBLE_STEPS if sources % ASSEMBLE_STEPS == 0 else 1
    per_step = sources // steps
    in_specs = [
        pl.BlockSpec((per_step, 2, tokens, r.shape[3]), lambda s: (s, 0, 0, 0)) for r in received
    ]
    out_spec = pl.BlockSpec((None, tokens, per_step * local_width), lambda s: (0, 0, s))
    return pl.pallas_call(
        assemble_kernel,
        grid=(steps,),
        in_specs=in_specs,
        out_specs=[out_spec, out_spec],
        out_shape=[
            jax.ShapeDtypeStruct((1, tokens, width), jnp.float32),
            jax.ShapeDtypeStruct((1, tokens, width), jnp.float32),
        ],
    )(*received)


def chunk_sizes(local_heads):
    if local_heads <= 2:
        return [1] * local_heads
    return [1, 1, local_heads - 2]


RESULT_DTYPE = jnp.bfloat16


def per_device_body(
    q_proj, q_tangent, k_proj, k_tangent, v_proj, v_tangent, query_norm_gain, key_norm_gain, lengths
):
    seq_count = lax.axis_size("seq")
    tokens = q_proj.shape[1]
    width = q_proj.shape[2]
    local_heads = width // HEAD_DIM // seq_count
    pack_tokens = tokens * seq_count
    sizes = chunk_sizes(local_heads)
    starts = [sum(sizes[:c]) for c in range(len(sizes))]

    assert tokens == BLOCK

    def by_destination(array, heads):
        split = array.reshape(tokens, seq_count, local_heads, HEAD_DIM)[:, :, heads]
        return jnp.transpose(split, (1, 2, 0, 3))

    value_payload = by_destination_all((v_proj, v_tangent), seq_count)
    values = lax.all_to_all(value_payload, "seq", split_axis=0, concat_axis=0, tiled=True)

    q_normed, dq_normed = normalize(q_proj, q_tangent, query_norm_gain)
    k_normed, dk_normed = normalize(k_proj, k_tangent, key_norm_gain)
    own_row = lax.dynamic_slice_in_dim(lengths, lax.axis_index("samp"), 1, 0)[0]
    first_block, last_block, sample_ends = block_tables(own_row, pack_tokens)
    normed = (q_normed, dq_normed, k_normed, dk_normed)
    results = []
    for first_head, chunk_heads in zip(starts, sizes):
        heads = slice(first_head, first_head + chunk_heads)
        payload = jnp.concatenate([by_destination(array, heads) for array in normed], axis=1)
        stacked = lax.all_to_all(payload, "seq", split_axis=0, concat_axis=0, tiled=True)
        result = attend(
            stacked, values, chunk_heads, first_head,
            first_block, last_block, sample_ends, RESULT_DTYPE,
        )
        results.append(result)
    received = []
    for members in (results[:2], results[2:]):
        if not members:
            continue
        group = jnp.concatenate(members, axis=3)
        received.append(lax.all_to_all(group, "seq", split_axis=0, concat_axis=0, tiled=True))
    return tuple(assemble(received, tokens, width))


def solution(mesh):
    placed = (
        P(("groups", "samp"), "seq", None),
        P(("groups", "samp"), "seq", None),
        P(("groups", "samp"), "seq", None),
        P(("groups", "samp"), "seq", None),
        P(("groups", "samp"), "seq", None),
        P(("groups", "samp"), "seq", None),
        P(),
        P(),
        P("groups", None),
    )
    return jax.shard_map(
        per_device_body,
        mesh=mesh,
        in_specs=placed,
        out_specs=(P(("groups", "samp"), "seq", None), P(("groups", "samp"), "seq", None)),
        check_vma=False,
    )
```

```python
import functools
import math

import jax
import jax.numpy as jnp
from jax import lax
from jax.experimental import pallas as pl
from jax.experimental.pallas import tpu as pltpu
from jax.sharding import PartitionSpec as P


HEAD_DIM = 128
BLOCK = 256
KEY_BLOCK = 256


def normalize(source, source_tangent, gain):
    widened = source.astype(jnp.float32)
    dwidened = source_tangent.astype(jnp.float32)
    inverse = lax.rsqrt(jnp.mean(widened * widened, axis=-1, keepdims=True) + 1e-06)
    radial = jnp.mean(widened * dwidened, axis=-1, keepdims=True)
    normed = (widened * inverse * gain).astype(jnp.bfloat16)
    tangent = ((dwidened * inverse - widened * inverse**3 * radial) * gain).astype(jnp.bfloat16)
    return (normed, tangent)


def block_tables(sample_lengths, count):
    sample_ends = jnp.cumsum(sample_lengths).astype(jnp.int32)
    sample_starts = sample_ends - sample_lengths
    blocks = count // BLOCK
    first_rows = jnp.arange(blocks, dtype=jnp.int32) * BLOCK
    last_rows = first_rows + (BLOCK - 1)
    first_segment = jnp.sum((first_rows[:, None] >= sample_ends[None, :]).astype(jnp.int32), axis=1)
    last_segment = jnp.sum((last_rows[:, None] >= sample_ends[None, :]).astype(jnp.int32), axis=1)
    samples = sample_lengths.shape[0]
    first_segment = jnp.clip(first_segment, 0, samples - 1)
    last_segment = jnp.clip(last_segment, 0, samples - 1)
    first_key = jnp.take(sample_starts, first_segment)
    last_key = jnp.take(sample_ends, last_segment)
    key_blocks = count // KEY_BLOCK
    first_block = jnp.clip(first_key // KEY_BLOCK, 0, key_blocks - 1)
    last_block = jnp.clip((last_key - 1) // KEY_BLOCK + 1, first_block + 1, key_blocks)
    return first_block.astype(jnp.int32), last_block.astype(jnp.int32), sample_ends


def attention_kernel(
    first_ref, last_ref, ends_ref,
    q_ref, dq_ref, k_ref, dk_ref, v_ref, dv_ref,
    result_ref,
):
    i = pl.program_id(1)
    samples = ends_ref.shape[0]
    factor = 1.0 / math.sqrt(HEAD_DIM)
    queries = q_ref[...]
    dqueries = dq_ref[...]
    both_queries = jnp.concatenate([dqueries, queries], axis=1)

    def segment_of(positions):
        seg = jnp.zeros(positions.shape, jnp.int32)
        for j in range(samples):
            seg = seg + (positions >= ends_ref[j]).astype(jnp.int32)
        return seg

    query_positions = i * BLOCK + lax.broadcasted_iota(jnp.int32, (BLOCK, 1), 0)
    query_segment = segment_of(query_positions)
    first = first_ref[i]
    last = last_ref[i]

    def scores_of(kb):
        start = kb * KEY_BLOCK
        key_rows = k_ref[kb]
        key_positions = start + lax.broadcasted_iota(jnp.int32, (1, KEY_BLOCK), 1)
        same = query_segment == segment_of(key_positions)
        raw = lax.dot_general(
            queries, key_rows, (((1,), (1,)), ((), ())), preferred_element_type=jnp.float32
        ) * factor
        return raw, same, start, key_rows

    def statistics(kb, carry):
        row_top, total = carry
        raw, same, _, _ = scores_of(kb)
        masked = jnp.where(same, raw, -1e30)
        new_top = jnp.maximum(row_top, jnp.max(masked, axis=1, keepdims=True))
        exponent = jnp.where(same, jnp.exp(masked - new_top), 0.0)
        total = total * jnp.exp(row_top - new_top) + jnp.sum(exponent, axis=1, keepdims=True)
        return new_top, total

    row_top, total = lax.fori_loop(
        first, last, statistics,
        (jnp.full((BLOCK, 1), -1e30, jnp.float32), jnp.zeros((BLOCK, 1), jnp.float32)),
    )
    inverse_total = 1.0 / total

    def sums(kb, carry):
        center, output, spread_sum, dvalue_sum = carry
        raw, same, _, key_rows = scores_of(kb)
        dkey_rows = dk_ref[kb]
        value_rows = v_ref[kb]
        dvalue_rows = dv_ref[kb]
        both_keys = jnp.concatenate([key_rows, dkey_rows], axis=1)
        dscores = lax.dot_general(
            both_queries, both_keys, (((1,), (1,)), ((), ())), preferred_element_type=jnp.float32
        ) * factor
        weights = jnp.where(same, jnp.exp(raw - row_top), 0.0) * inverse_total
        product = jnp.where(same, weights * dscores, 0.0)
        center = center + jnp.sum(product, axis=1, keepdims=True)
        rounded = weights.astype(jnp.bfloat16)
        spread = product.astype(jnp.bfloat16)
        output = output + jnp.dot(rounded, value_rows, preferred_element_type=jnp.float32)
        spread_sum = spread_sum + jnp.dot(spread, value_rows, preferred_element_type=jnp.float32)
        dvalue_sum = dvalue_sum + jnp.dot(rounded, dvalue_rows, preferred_element_type=jnp.float32)
        return center, output, spread_sum, dvalue_sum

    empty = jnp.zeros((BLOCK, HEAD_DIM), jnp.float32)
    center, output, spread_sum, dvalue_sum = lax.fori_loop(
        first, last, sums, (jnp.zeros((BLOCK, 1), jnp.float32), empty, empty, empty)
    )
    result_ref[0] = output.astype(result_ref.dtype)
    result_ref[1] = (spread_sum - center * output + dvalue_sum).astype(result_ref.dtype)


def attend(stacked, values, heads, offset, first_block, last_block, sample_ends, result_dtype):
    sources = stacked.shape[0]
    all_heads = values.shape[1] // 2

    def query_spec(t):
        return pl.BlockSpec((None, None, BLOCK, HEAD_DIM), lambda h, i, *_: (i, t * heads + h, 0, 0))

    def key_spec(t):
        return pl.BlockSpec((sources, None, BLOCK, HEAD_DIM), lambda h, i, *_: (0, t * heads + h, 0, 0))

    def value_spec(t):
        return pl.BlockSpec(
            (sources, None, BLOCK, HEAD_DIM), lambda h, i, *_: (0, t * all_heads + offset + h, 0, 0)
        )

    grid_spec = pltpu.PrefetchScalarGridSpec(
        num_scalar_prefetch=3,
        grid=(heads, sources),
        in_specs=[query_spec(0), query_spec(1), key_spec(2), key_spec(3), value_spec(0), value_spec(1)],
        out_specs=pl.BlockSpec((None, 2, BLOCK, HEAD_DIM), lambda h, i, *_: (i, 0, 0, h)),
    )
    return pl.pallas_call(
        attention_kernel,
        grid_spec=grid_spec,
        out_shape=jax.ShapeDtypeStruct((sources, 2, BLOCK, heads * HEAD_DIM), result_dtype),
        compiler_params=pltpu.CompilerParams(
            dimension_semantics=("arbitrary", "arbitrary"),
        ),
    )(first_block, last_block, sample_ends, stacked, stacked, stacked, stacked, values, values)


def gather_kernel(*refs):
    *sources, out_ref = refs
    per_step = out_ref.shape[0]
    heads = out_ref.shape[1] // len(sources)
    for d in range(per_step):
        for t, ref in enumerate(sources):
            for h in range(heads):
                column = (d * heads + h) * HEAD_DIM
                out_ref[d, t * heads + h] = ref[:, column:column + HEAD_DIM]


GATHER_STEPS = 2


def by_destination_all(arrays, destinations):
    tokens, width = arrays[0].shape[1], arrays[0].shape[2]
    local_width = width // destinations
    heads = local_width // HEAD_DIM
    steps = GATHER_STEPS if destinations % GATHER_STEPS == 0 else 1
    per_step = destinations // steps
    in_spec = pl.BlockSpec((None, tokens, per_step * local_width), lambda d: (0, 0, d))
    return pl.pallas_call(
        gather_kernel,
        grid=(steps,),
        in_specs=[in_spec] * len(arrays),
        out_specs=pl.BlockSpec(
            (per_step, len(arrays) * heads, tokens, HEAD_DIM), lambda d: (d, 0, 0, 0)
        ),
        out_shape=jax.ShapeDtypeStruct(
            (destinations, len(arrays) * heads, tokens, HEAD_DIM), arrays[0].dtype
        ),
    )(*arrays)


def assemble_kernel(part, parts, received_ref, *refs):
    out_ref, tan_ref, staged, widened, load_sem, store_sems = refs[-6:]
    sources, _, _, part_width = staged.shape
    local_width = part_width * parts
    load = pltpu.make_async_copy(received_ref, staged, load_sem)
    load.start()
    load.wait()
    stores = []
    for s in range(sources):
        column = s * local_width + part * part_width
        for p, target in enumerate((out_ref, tan_ref)):
            widened[p, s] = staged[s, p].astype(jnp.float32)
            store = pltpu.make_async_copy(
                widened.at[p, s], target.at[0, :, pl.ds(column, part_width)], store_sems.at[p, s]
            )
            store.start()
            stores.append(store)
    for store in stores:
        store.wait()


def assemble_part(received, part, parts, previous, tokens, width):
    sources, _, _, part_width = received.shape
    operands = [received]
    aliases = {}
    if previous is not None:
        operands += list(previous)
        aliases = {1: 0, 2: 1}
    return pl.pallas_call(
        functools.partial(assemble_kernel, part, parts),
        in_specs=[pl.BlockSpec(memory_space=pl.ANY)] * len(operands),
        out_specs=[pl.BlockSpec(memory_space=pl.ANY), pl.BlockSpec(memory_space=pl.ANY)],
        out_shape=[
            jax.ShapeDtypeStruct((1, tokens, width), jnp.float32),
            jax.ShapeDtypeStruct((1, tokens, width), jnp.float32),
        ],
        scratch_shapes=[
            pltpu.VMEM((sources, 2, tokens, part_width), received.dtype),
            pltpu.VMEM((2, sources, tokens, part_width), jnp.float32),
            pltpu.SemaphoreType.DMA(()),
            pltpu.SemaphoreType.DMA((2, sources)),
        ],
        input_output_aliases=aliases,
    )(*operands)


CHUNKS = 4
RESULT_DTYPE = jnp.bfloat16


def per_device_body(
    q_proj, q_tangent, k_proj, k_tangent, v_proj, v_tangent, query_norm_gain, key_norm_gain, lengths
):
    seq_count = lax.axis_size("seq")
    tokens = q_proj.shape[1]
    width = q_proj.shape[2]
    local_heads = width // HEAD_DIM // seq_count
    pack_tokens = tokens * seq_count
    chunks = min(CHUNKS, local_heads)
    chunk_heads = local_heads // chunks

    assert tokens == BLOCK

    def by_destination(array, heads):
        split = array.reshape(tokens, seq_count, local_heads, HEAD_DIM)[:, :, heads]
        return jnp.transpose(split, (1, 2, 0, 3))

    value_payload = by_destination_all((v_proj, v_tangent), seq_count)
    values = lax.all_to_all(value_payload, "seq", split_axis=0, concat_axis=0, tiled=True)

    q_normed, dq_normed = normalize(q_proj, q_tangent, query_norm_gain)
    k_normed, dk_normed = normalize(k_proj, k_tangent, key_norm_gain)
    own_row = lax.dynamic_slice_in_dim(lengths, lax.axis_index("samp"), 1, 0)[0]
    first_block, last_block, sample_ends = block_tables(own_row, pack_tokens)
    normed = (q_normed, dq_normed, k_normed, dk_normed)
    results = []
    for c in range(chunks):
        heads = slice(c * chunk_heads, (c + 1) * chunk_heads)
        payload = jnp.concatenate([by_destination(array, heads) for array in normed], axis=1)
        stacked = lax.all_to_all(payload, "seq", split_axis=0, concat_axis=0, tiled=True)
        result = attend(
            stacked, values, chunk_heads, c * chunk_heads,
            first_block, last_block, sample_ends, RESULT_DTYPE,
        )
        results.append(result)
    groups = [results[g:g + 2] for g in range(0, len(results), 2)]
    outputs = None
    for g, members in enumerate(groups):
        group = jnp.concatenate(members, axis=3)
        received = lax.all_to_all(group, "seq", split_axis=0, concat_axis=0, tiled=True)
        outputs = assemble_part(received, g, len(groups), outputs, tokens, width)
    return tuple(outputs)


def solution(mesh):
    placed = (
        P(("groups", "samp"), "seq", None),
        P(("groups", "samp"), "seq", None),
        P(("groups", "samp"), "seq", None),
        P(("groups", "samp"), "seq", None),
        P(("groups", "samp"), "seq", None),
        P(("groups", "samp"), "seq", None),
        P(),
        P(),
        P("groups", None),
    )
    return jax.shard_map(
        per_device_body,
        mesh=mesh,
        in_specs=placed,
        out_specs=(P(("groups", "samp"), "seq", None), P(("groups", "samp"), "seq", None)),
        check_vma=False,
    )
```

```python
import math

import jax
import jax.numpy as jnp
from jax import lax
from jax.experimental import pallas as pl
from jax.experimental.pallas import tpu as pltpu
from jax.sharding import PartitionSpec as P


HEAD_DIM = 128
BLOCK = 256
KEY_BLOCK = 256


def normalize(source, source_tangent, gain):
    widened = source.astype(jnp.float32)
    dwidened = source_tangent.astype(jnp.float32)
    inverse = lax.rsqrt(jnp.mean(widened * widened, axis=-1, keepdims=True) + 1e-06)
    radial = jnp.mean(widened * dwidened, axis=-1, keepdims=True)
    normed = (widened * inverse * gain).astype(jnp.bfloat16)
    tangent = ((dwidened * inverse - widened * inverse**3 * radial) * gain).astype(jnp.bfloat16)
    return (normed, tangent)


def block_tables(sample_lengths, count):
    sample_ends = jnp.cumsum(sample_lengths).astype(jnp.int32)
    sample_starts = sample_ends - sample_lengths
    blocks = count // BLOCK
    first_rows = jnp.arange(blocks, dtype=jnp.int32) * BLOCK
    last_rows = first_rows + (BLOCK - 1)
    first_segment = jnp.sum((first_rows[:, None] >= sample_ends[None, :]).astype(jnp.int32), axis=1)
    last_segment = jnp.sum((last_rows[:, None] >= sample_ends[None, :]).astype(jnp.int32), axis=1)
    samples = sample_lengths.shape[0]
    first_segment = jnp.clip(first_segment, 0, samples - 1)
    last_segment = jnp.clip(last_segment, 0, samples - 1)
    first_key = jnp.take(sample_starts, first_segment)
    last_key = jnp.take(sample_ends, last_segment)
    key_blocks = count // KEY_BLOCK
    first_block = jnp.clip(first_key // KEY_BLOCK, 0, key_blocks - 1)
    last_block = jnp.clip((last_key - 1) // KEY_BLOCK + 1, first_block + 1, key_blocks)
    return first_block.astype(jnp.int32), last_block.astype(jnp.int32), sample_ends


def attention_kernel(
    first_ref, last_ref, ends_ref,
    q_ref, dq_ref, k_ref, dk_ref, v_ref, dv_ref,
    result_ref,
):
    i = pl.program_id(1)
    samples = ends_ref.shape[0]
    factor = 1.0 / math.sqrt(HEAD_DIM)
    queries = q_ref[...]
    dqueries = dq_ref[...]
    both_queries = jnp.concatenate([dqueries, queries], axis=1)

    def segment_of(positions):
        seg = jnp.zeros(positions.shape, jnp.int32)
        for j in range(samples):
            seg = seg + (positions >= ends_ref[j]).astype(jnp.int32)
        return seg

    query_positions = i * BLOCK + lax.broadcasted_iota(jnp.int32, (BLOCK, 1), 0)
    query_segment = segment_of(query_positions)
    first = first_ref[i]
    last = last_ref[i]

    def scores_of(kb):
        start = kb * KEY_BLOCK
        key_rows = k_ref[kb]
        key_positions = start + lax.broadcasted_iota(jnp.int32, (1, KEY_BLOCK), 1)
        same = query_segment == segment_of(key_positions)
        raw = lax.dot_general(
            queries, key_rows, (((1,), (1,)), ((), ())), preferred_element_type=jnp.float32
        ) * factor
        return raw, same, start, key_rows

    def statistics(kb, carry):
        row_top, total = carry
        raw, same, _, _ = scores_of(kb)
        masked = jnp.where(same, raw, -1e30)
        new_top = jnp.maximum(row_top, jnp.max(masked, axis=1, keepdims=True))
        exponent = jnp.where(same, jnp.exp(masked - new_top), 0.0)
        total = total * jnp.exp(row_top - new_top) + jnp.sum(exponent, axis=1, keepdims=True)
        return new_top, total

    row_top, total = lax.fori_loop(
        first, last, statistics,
        (jnp.full((BLOCK, 1), -1e30, jnp.float32), jnp.zeros((BLOCK, 1), jnp.float32)),
    )
    inverse_total = 1.0 / total

    def sums(kb, carry):
        center, output, spread_sum, dvalue_sum = carry
        raw, same, _, key_rows = scores_of(kb)
        dkey_rows = dk_ref[kb]
        value_rows = v_ref[kb]
        dvalue_rows = dv_ref[kb]
        both_keys = jnp.concatenate([key_rows, dkey_rows], axis=1)
        dscores = lax.dot_general(
            both_queries, both_keys, (((1,), (1,)), ((), ())), preferred_element_type=jnp.float32
        ) * factor
        weights = jnp.where(same, jnp.exp(raw - row_top), 0.0) * inverse_total
        product = jnp.where(same, weights * dscores, 0.0)
        center = center + jnp.sum(product, axis=1, keepdims=True)
        rounded = weights.astype(jnp.bfloat16)
        spread = product.astype(jnp.bfloat16)
        output = output + jnp.dot(rounded, value_rows, preferred_element_type=jnp.float32)
        spread_sum = spread_sum + jnp.dot(spread, value_rows, preferred_element_type=jnp.float32)
        dvalue_sum = dvalue_sum + jnp.dot(rounded, dvalue_rows, preferred_element_type=jnp.float32)
        return center, output, spread_sum, dvalue_sum

    empty = jnp.zeros((BLOCK, HEAD_DIM), jnp.float32)
    center, output, spread_sum, dvalue_sum = lax.fori_loop(
        first, last, sums, (jnp.zeros((BLOCK, 1), jnp.float32), empty, empty, empty)
    )
    result_ref[0] = output.astype(result_ref.dtype)
    result_ref[1] = (spread_sum - center * output + dvalue_sum).astype(result_ref.dtype)


def attend(stacked, values, heads, offset, first_block, last_block, sample_ends, result_dtype):
    sources = stacked.shape[0]
    all_heads = values.shape[1] // 2

    def query_spec(t):
        return pl.BlockSpec((None, None, BLOCK, HEAD_DIM), lambda h, i, *_: (i, t * heads + h, 0, 0))

    def key_spec(t):
        return pl.BlockSpec((sources, None, BLOCK, HEAD_DIM), lambda h, i, *_: (0, t * heads + h, 0, 0))

    def value_spec(t):
        return pl.BlockSpec(
            (sources, None, BLOCK, HEAD_DIM), lambda h, i, *_: (0, t * all_heads + offset + h, 0, 0)
        )

    grid_spec = pltpu.PrefetchScalarGridSpec(
        num_scalar_prefetch=3,
        grid=(heads, sources),
        in_specs=[query_spec(0), query_spec(1), key_spec(2), key_spec(3), value_spec(0), value_spec(1)],
        out_specs=pl.BlockSpec((None, 2, BLOCK, HEAD_DIM), lambda h, i, *_: (i, 0, 0, h)),
    )
    return pl.pallas_call(
        attention_kernel,
        grid_spec=grid_spec,
        out_shape=jax.ShapeDtypeStruct((sources, 2, BLOCK, heads * HEAD_DIM), result_dtype),
        compiler_params=pltpu.CompilerParams(
            dimension_semantics=("arbitrary", "arbitrary"),
        ),
    )(first_block, last_block, sample_ends, stacked, stacked, stacked, stacked, values, values)


def assemble_kernel(*refs):
    *received, out_ref, tan_ref = refs
    per_step = received[0].shape[0]
    local_width = out_ref.shape[1] // per_step
    for s in range(per_step):
        offset = s * local_width
        for r in received:
            w = r.shape[-1]
            out_ref[:, offset:offset + w] = r[s, 0].astype(jnp.float32)
            tan_ref[:, offset:offset + w] = r[s, 1].astype(jnp.float32)
            offset += w


ASSEMBLE_STEPS = 2


def assemble(received, tokens, width):
    sources = received[0].shape[0]
    local_width = width // sources
    steps = ASSEMBLE_STEPS if sources % ASSEMBLE_STEPS == 0 else 1
    per_step = sources // steps
    in_specs = [
        pl.BlockSpec((per_step, 2, tokens, r.shape[3]), lambda s: (s, 0, 0, 0)) for r in received
    ]
    out_spec = pl.BlockSpec((None, tokens, per_step * local_width), lambda s: (0, 0, s))
    return pl.pallas_call(
        assemble_kernel,
        grid=(steps,),
        in_specs=in_specs,
        out_specs=[out_spec, out_spec],
        out_shape=[
            jax.ShapeDtypeStruct((1, tokens, width), jnp.float32),
            jax.ShapeDtypeStruct((1, tokens, width), jnp.float32),
        ],
    )(*received)


CHUNKS = 4
RESULT_DTYPE = jnp.bfloat16


def per_device_body(
    q_proj, q_tangent, k_proj, k_tangent, v_proj, v_tangent, query_norm_gain, key_norm_gain, lengths
):
    seq_count = lax.axis_size("seq")
    tokens = q_proj.shape[1]
    width = q_proj.shape[2]
    local_heads = width // HEAD_DIM // seq_count
    pack_tokens = tokens * seq_count
    chunks = min(CHUNKS, local_heads)
    chunk_heads = local_heads // chunks

    assert tokens == BLOCK

    def by_destination(array, heads):
        split = array.reshape(tokens, seq_count, local_heads, HEAD_DIM)[:, :, heads]
        return jnp.transpose(split, (1, 2, 0, 3))

    me = lax.axis_index("seq")
    local_width = local_heads * HEAD_DIM
    both = jnp.stack(
        [array.reshape(tokens, seq_count, local_width) for array in (v_proj, v_tangent)], axis=0
    )
    pieces = [lax.dynamic_index_in_dim(both, me, 2, keepdims=False)]
    for d in range(1, seq_count):
        piece = lax.dynamic_index_in_dim(both, (me + d) % seq_count, 2, keepdims=False)
        pieces.append(lax.ppermute(
            piece, "seq", [(s, (s + d) % seq_count) for s in range(seq_count)]
        ))
    by_shift = jnp.stack(pieces, axis=0)
    order = (me - jnp.arange(seq_count, dtype=jnp.int32)) % seq_count
    by_source = jnp.take(by_shift, order, axis=0)
    values = jnp.transpose(
        by_source.reshape(seq_count, 2, tokens, local_heads, HEAD_DIM), (0, 1, 3, 2, 4)
    ).reshape(seq_count, 2 * local_heads, tokens, HEAD_DIM)

    q_normed, dq_normed = normalize(q_proj, q_tangent, query_norm_gain)
    k_normed, dk_normed = normalize(k_proj, k_tangent, key_norm_gain)
    own_row = lax.dynamic_slice_in_dim(lengths, lax.axis_index("samp"), 1, 0)[0]
    first_block, last_block, sample_ends = block_tables(own_row, pack_tokens)
    normed = (q_normed, dq_normed, k_normed, dk_normed)
    results = []
    for c in range(chunks):
        heads = slice(c * chunk_heads, (c + 1) * chunk_heads)
        payload = jnp.concatenate([by_destination(array, heads) for array in normed], axis=1)
        stacked = lax.all_to_all(payload, "seq", split_axis=0, concat_axis=0, tiled=True)
        result = attend(
            stacked, values, chunk_heads, c * chunk_heads,
            first_block, last_block, sample_ends, RESULT_DTYPE,
        )
        results.append(result)
    received = []
    for g in range(0, chunks, 2):
        group = jnp.concatenate(results[g:g + 2], axis=3)
        received.append(lax.all_to_all(group, "seq", split_axis=0, concat_axis=0, tiled=True))
    return tuple(assemble(received, tokens, width))


def solution(mesh):
    placed = (
        P(("groups", "samp"), "seq", None),
        P(("groups", "samp"), "seq", None),
        P(("groups", "samp"), "seq", None),
        P(("groups", "samp"), "seq", None),
        P(("groups", "samp"), "seq", None),
        P(("groups", "samp"), "seq", None),
        P(),
        P(),
        P("groups", None),
    )
    return jax.shard_map(
        per_device_body,
        mesh=mesh,
        in_specs=placed,
        out_specs=(P(("groups", "samp"), "seq", None), P(("groups", "samp"), "seq", None)),
        check_vma=False,
    )
```

```python
import math

import jax
import jax.numpy as jnp
from jax import lax
from jax.experimental import pallas as pl
from jax.experimental.pallas import tpu as pltpu
from jax.sharding import PartitionSpec as P


HEAD_DIM = 128
BLOCK = 256
KEY_BLOCK = 256


def normalize(source, source_tangent, gain):
    widened = source.astype(jnp.float32)
    dwidened = source_tangent.astype(jnp.float32)
    inverse = lax.rsqrt(jnp.mean(widened * widened, axis=-1, keepdims=True) + 1e-06)
    radial = jnp.mean(widened * dwidened, axis=-1, keepdims=True)
    normed = (widened * inverse * gain).astype(jnp.bfloat16)
    tangent = ((dwidened * inverse - widened * inverse**3 * radial) * gain).astype(jnp.bfloat16)
    return (normed, tangent)


def block_tables(sample_lengths, count):
    sample_ends = jnp.cumsum(sample_lengths).astype(jnp.int32)
    sample_starts = sample_ends - sample_lengths
    blocks = count // BLOCK
    first_rows = jnp.arange(blocks, dtype=jnp.int32) * BLOCK
    last_rows = first_rows + (BLOCK - 1)
    first_segment = jnp.sum((first_rows[:, None] >= sample_ends[None, :]).astype(jnp.int32), axis=1)
    last_segment = jnp.sum((last_rows[:, None] >= sample_ends[None, :]).astype(jnp.int32), axis=1)
    samples = sample_lengths.shape[0]
    first_segment = jnp.clip(first_segment, 0, samples - 1)
    last_segment = jnp.clip(last_segment, 0, samples - 1)
    first_key = jnp.take(sample_starts, first_segment)
    last_key = jnp.take(sample_ends, last_segment)
    key_blocks = count // KEY_BLOCK
    first_block = jnp.clip(first_key // KEY_BLOCK, 0, key_blocks - 1)
    last_block = jnp.clip((last_key - 1) // KEY_BLOCK + 1, first_block + 1, key_blocks)
    return first_block.astype(jnp.int32), last_block.astype(jnp.int32), sample_ends


def attention_kernel(
    first_ref, last_ref, ends_ref,
    q_ref, dq_ref, k_ref, dk_ref, v_ref, dv_ref,
    result_ref,
):
    i = pl.program_id(1)
    samples = ends_ref.shape[0]
    factor = 1.0 / math.sqrt(HEAD_DIM)
    queries = q_ref[...]
    dqueries = dq_ref[...]
    both_queries = jnp.concatenate([dqueries, queries], axis=1)

    def segment_of(positions):
        seg = jnp.zeros(positions.shape, jnp.int32)
        for j in range(samples):
            seg = seg + (positions >= ends_ref[j]).astype(jnp.int32)
        return seg

    query_positions = i * BLOCK + lax.broadcasted_iota(jnp.int32, (BLOCK, 1), 0)
    query_segment = segment_of(query_positions)
    first = first_ref[i]
    last = last_ref[i]

    def scores_of(kb):
        start = kb * KEY_BLOCK
        key_rows = k_ref[kb]
        key_positions = start + lax.broadcasted_iota(jnp.int32, (1, KEY_BLOCK), 1)
        same = query_segment == segment_of(key_positions)
        raw = lax.dot_general(
            queries, key_rows, (((1,), (1,)), ((), ())), preferred_element_type=jnp.float32
        ) * factor
        return raw, same, start, key_rows

    def statistics(kb, carry):
        row_top, total = carry
        raw, same, _, _ = scores_of(kb)
        masked = jnp.where(same, raw, -1e30)
        new_top = jnp.maximum(row_top, jnp.max(masked, axis=1, keepdims=True))
        exponent = jnp.where(same, jnp.exp(masked - new_top), 0.0)
        total = total * jnp.exp(row_top - new_top) + jnp.sum(exponent, axis=1, keepdims=True)
        return new_top, total

    row_top, total = lax.fori_loop(
        first, last, statistics,
        (jnp.full((BLOCK, 1), -1e30, jnp.float32), jnp.zeros((BLOCK, 1), jnp.float32)),
    )
    inverse_total = 1.0 / total

    def sums(kb, carry):
        center, output, spread_sum, dvalue_sum = carry
        raw, same, _, key_rows = scores_of(kb)
        dkey_rows = dk_ref[kb]
        value_rows = v_ref[kb]
        dvalue_rows = dv_ref[kb]
        both_keys = jnp.concatenate([key_rows, dkey_rows], axis=1)
        dscores = lax.dot_general(
            both_queries, both_keys, (((1,), (1,)), ((), ())), preferred_element_type=jnp.float32
        ) * factor
        weights = jnp.where(same, jnp.exp(raw - row_top), 0.0) * inverse_total
        product = jnp.where(same, weights * dscores, 0.0)
        center = center + jnp.sum(product, axis=1, keepdims=True)
        rounded = weights.astype(jnp.bfloat16)
        spread = product.astype(jnp.bfloat16)
        output = output + jnp.dot(rounded, value_rows, preferred_element_type=jnp.float32)
        spread_sum = spread_sum + jnp.dot(spread, value_rows, preferred_element_type=jnp.float32)
        dvalue_sum = dvalue_sum + jnp.dot(rounded, dvalue_rows, preferred_element_type=jnp.float32)
        return center, output, spread_sum, dvalue_sum

    empty = jnp.zeros((BLOCK, HEAD_DIM), jnp.float32)
    center, output, spread_sum, dvalue_sum = lax.fori_loop(
        first, last, sums, (jnp.zeros((BLOCK, 1), jnp.float32), empty, empty, empty)
    )
    result_ref[0] = output.astype(result_ref.dtype)
    result_ref[1] = (spread_sum - center * output + dvalue_sum).astype(result_ref.dtype)


def attend(stacked, values, heads, offset, first_block, last_block, sample_ends, result_dtype):
    sources = stacked.shape[0]
    all_heads = values.shape[1] // 2

    def query_spec(t):
        return pl.BlockSpec((None, None, BLOCK, HEAD_DIM), lambda h, i, *_: (i, t * heads + h, 0, 0))

    def key_spec(t):
        return pl.BlockSpec((sources, None, BLOCK, HEAD_DIM), lambda h, i, *_: (0, t * heads + h, 0, 0))

    def value_spec(t):
        return pl.BlockSpec(
            (sources, None, BLOCK, HEAD_DIM), lambda h, i, *_: (0, t * all_heads + offset + h, 0, 0)
        )

    grid_spec = pltpu.PrefetchScalarGridSpec(
        num_scalar_prefetch=3,
        grid=(heads, sources),
        in_specs=[query_spec(0), query_spec(1), key_spec(2), key_spec(3), value_spec(0), value_spec(1)],
        out_specs=pl.BlockSpec((None, 2, BLOCK, HEAD_DIM), lambda h, i, *_: (i, 0, 0, h)),
    )
    return pl.pallas_call(
        attention_kernel,
        grid_spec=grid_spec,
        out_shape=jax.ShapeDtypeStruct((sources, 2, BLOCK, heads * HEAD_DIM), result_dtype),
        compiler_params=pltpu.CompilerParams(
            dimension_semantics=("arbitrary", "arbitrary"),
        ),
    )(first_block, last_block, sample_ends, stacked, stacked, stacked, stacked, values, values)


def gather_kernel(*refs):
    *sources, out_ref = refs
    per_step = out_ref.shape[0]
    heads = out_ref.shape[1] // len(sources)
    for d in range(per_step):
        for t, ref in enumerate(sources):
            for h in range(heads):
                column = (d * heads + h) * HEAD_DIM
                out_ref[d, t * heads + h] = ref[:, column:column + HEAD_DIM]


GATHER_STEPS = 2


def by_destination_all(arrays, destinations):
    tokens, width = arrays[0].shape[1], arrays[0].shape[2]
    local_width = width // destinations
    heads = local_width // HEAD_DIM
    steps = GATHER_STEPS if destinations % GATHER_STEPS == 0 else 1
    per_step = destinations // steps
    in_spec = pl.BlockSpec((None, tokens, per_step * local_width), lambda d: (0, 0, d))
    return pl.pallas_call(
        gather_kernel,
        grid=(steps,),
        in_specs=[in_spec] * len(arrays),
        out_specs=pl.BlockSpec(
            (per_step, len(arrays) * heads, tokens, HEAD_DIM), lambda d: (d, 0, 0, 0)
        ),
        out_shape=jax.ShapeDtypeStruct(
            (destinations, len(arrays) * heads, tokens, HEAD_DIM), arrays[0].dtype
        ),
    )(*arrays)


def assemble_kernel(*refs):
    *received, out_ref, tan_ref = refs
    per_step = received[0].shape[0]
    local_width = out_ref.shape[1] // per_step
    for s in range(per_step):
        offset = s * local_width
        for r in received:
            w = r.shape[-1]
            out_ref[:, offset:offset + w] = r[s, 0].astype(jnp.float32)
            tan_ref[:, offset:offset + w] = r[s, 1].astype(jnp.float32)
            offset += w


ASSEMBLE_STEPS = 2


def assemble(received, tokens, width):
    sources = received[0].shape[0]
    local_width = width // sources
    steps = ASSEMBLE_STEPS if sources % ASSEMBLE_STEPS == 0 else 1
    per_step = sources // steps
    in_specs = [
        pl.BlockSpec((per_step, 2, tokens, r.shape[3]), lambda s: (s, 0, 0, 0)) for r in received
    ]
    out_spec = pl.BlockSpec((None, tokens, per_step * local_width), lambda s: (0, 0, s))
    return pl.pallas_call(
        assemble_kernel,
        grid=(steps,),
        in_specs=in_specs,
        out_specs=[out_spec, out_spec],
        out_shape=[
            jax.ShapeDtypeStruct((1, tokens, width), jnp.float32),
            jax.ShapeDtypeStruct((1, tokens, width), jnp.float32),
        ],
    )(*received)


CHUNKS = 4
RESULT_DTYPE = jnp.bfloat16


def per_device_body(
    q_proj, q_tangent, k_proj, k_tangent, v_proj, v_tangent, query_norm_gain, key_norm_gain, lengths
):
    seq_count = lax.axis_size("seq")
    tokens = q_proj.shape[1]
    width = q_proj.shape[2]
    local_heads = width // HEAD_DIM // seq_count
    pack_tokens = tokens * seq_count
    chunks = min(CHUNKS, local_heads)
    chunk_heads = local_heads // chunks

    assert tokens == BLOCK

    def by_destination(array, heads):
        split = array.reshape(tokens, seq_count, local_heads, HEAD_DIM)[:, :, heads]
        return jnp.transpose(split, (1, 2, 0, 3))

    value_payload = by_destination_all((v_proj, v_tangent), seq_count)
    values = lax.all_to_all(value_payload, "seq", split_axis=0, concat_axis=0, tiled=True)

    q_normed, dq_normed = normalize(q_proj, q_tangent, query_norm_gain)
    k_normed, dk_normed = normalize(k_proj, k_tangent, key_norm_gain)
    shared = lax.ppermute(lengths, "seq", [(s, (s + 1) % seq_count) for s in range(seq_count)])
    own_row = lax.dynamic_slice_in_dim(shared, lax.axis_index("samp"), 1, 0)[0]
    first_block, last_block, sample_ends = block_tables(own_row, pack_tokens)
    normed = (q_normed, dq_normed, k_normed, dk_normed)
    results = []
    for c in range(chunks):
        heads = slice(c * chunk_heads, (c + 1) * chunk_heads)
        payload = jnp.concatenate([by_destination(array, heads) for array in normed], axis=1)
        stacked = lax.all_to_all(payload, "seq", split_axis=0, concat_axis=0, tiled=True)
        result = attend(
            stacked, values, chunk_heads, c * chunk_heads,
            first_block, last_block, sample_ends, RESULT_DTYPE,
        )
        results.append(result)
    received = []
    for g in range(0, chunks, 2):
        group = jnp.concatenate(results[g:g + 2], axis=3)
        received.append(lax.all_to_all(group, "seq", split_axis=0, concat_axis=0, tiled=True))
    return tuple(assemble(received, tokens, width))


def solution(mesh):
    placed = (
        P(("groups", "samp"), "seq", None),
        P(("groups", "samp"), "seq", None),
        P(("groups", "samp"), "seq", None),
        P(("groups", "samp"), "seq", None),
        P(("groups", "samp"), "seq", None),
        P(("groups", "samp"), "seq", None),
        P(),
        P(),
        P("groups", None),
    )
    return jax.shard_map(
        per_device_body,
        mesh=mesh,
        in_specs=placed,
        out_specs=(P(("groups", "samp"), "seq", None), P(("groups", "samp"), "seq", None)),
        check_vma=False,
    )
```

```python
import functools
import math

import jax
import jax.numpy as jnp
from jax import lax
from jax.experimental import pallas as pl
from jax.experimental.pallas import tpu as pltpu
from jax.sharding import PartitionSpec as P


HEAD_DIM = 128
BLOCK = 256
KEY_BLOCK = 256


def normalize(source, source_tangent, gain):
    widened = source.astype(jnp.float32)
    dwidened = source_tangent.astype(jnp.float32)
    inverse = lax.rsqrt(jnp.mean(widened * widened, axis=-1, keepdims=True) + 1e-06)
    radial = jnp.mean(widened * dwidened, axis=-1, keepdims=True)
    normed = (widened * inverse * gain).astype(jnp.bfloat16)
    tangent = ((dwidened * inverse - widened * inverse**3 * radial) * gain).astype(jnp.bfloat16)
    return (normed, tangent)


def block_tables(sample_lengths, count):
    sample_ends = jnp.cumsum(sample_lengths).astype(jnp.int32)
    sample_starts = sample_ends - sample_lengths
    blocks = count // BLOCK
    first_rows = jnp.arange(blocks, dtype=jnp.int32) * BLOCK
    last_rows = first_rows + (BLOCK - 1)
    first_segment = jnp.sum((first_rows[:, None] >= sample_ends[None, :]).astype(jnp.int32), axis=1)
    last_segment = jnp.sum((last_rows[:, None] >= sample_ends[None, :]).astype(jnp.int32), axis=1)
    samples = sample_lengths.shape[0]
    first_segment = jnp.clip(first_segment, 0, samples - 1)
    last_segment = jnp.clip(last_segment, 0, samples - 1)
    first_key = jnp.take(sample_starts, first_segment)
    last_key = jnp.take(sample_ends, last_segment)
    key_blocks = count // KEY_BLOCK
    first_block = jnp.clip(first_key // KEY_BLOCK, 0, key_blocks - 1)
    last_block = jnp.clip((last_key - 1) // KEY_BLOCK + 1, first_block + 1, key_blocks)
    return first_block.astype(jnp.int32), last_block.astype(jnp.int32), sample_ends


def attention_kernel(
    first_ref, last_ref, ends_ref,
    q_ref, dq_ref, k_ref, dk_ref, v_ref, dv_ref,
    result_ref,
):
    i = pl.program_id(1)
    samples = ends_ref.shape[0]
    factor = 1.0 / math.sqrt(HEAD_DIM)
    queries = q_ref[...]
    dqueries = dq_ref[...]
    both_queries = jnp.concatenate([dqueries, queries], axis=1)

    def segment_of(positions):
        seg = jnp.zeros(positions.shape, jnp.int32)
        for j in range(samples):
            seg = seg + (positions >= ends_ref[j]).astype(jnp.int32)
        return seg

    query_positions = i * BLOCK + lax.broadcasted_iota(jnp.int32, (BLOCK, 1), 0)
    query_segment = segment_of(query_positions)
    first = first_ref[i]
    last = last_ref[i]

    def scores_of(kb):
        start = kb * KEY_BLOCK
        key_rows = k_ref[kb]
        key_positions = start + lax.broadcasted_iota(jnp.int32, (1, KEY_BLOCK), 1)
        same = query_segment == segment_of(key_positions)
        raw = lax.dot_general(
            queries, key_rows, (((1,), (1,)), ((), ())), preferred_element_type=jnp.float32
        ) * factor
        return raw, same, start, key_rows

    def statistics(kb, carry):
        row_top, total = carry
        raw, same, _, _ = scores_of(kb)
        masked = jnp.where(same, raw, -1e30)
        new_top = jnp.maximum(row_top, jnp.max(masked, axis=1, keepdims=True))
        exponent = jnp.where(same, jnp.exp(masked - new_top), 0.0)
        total = total * jnp.exp(row_top - new_top) + jnp.sum(exponent, axis=1, keepdims=True)
        return new_top, total

    row_top, total = lax.fori_loop(
        first, last, statistics,
        (jnp.full((BLOCK, 1), -1e30, jnp.float32), jnp.zeros((BLOCK, 1), jnp.float32)),
    )
    inverse_total = 1.0 / total

    def sums(kb, carry):
        center, output, spread_sum, dvalue_sum = carry
        raw, same, _, key_rows = scores_of(kb)
        dkey_rows = dk_ref[kb]
        value_rows = v_ref[kb]
        dvalue_rows = dv_ref[kb]
        both_keys = jnp.concatenate([key_rows, dkey_rows], axis=1)
        dscores = lax.dot_general(
            both_queries, both_keys, (((1,), (1,)), ((), ())), preferred_element_type=jnp.float32
        ) * factor
        weights = jnp.where(same, jnp.exp(raw - row_top), 0.0) * inverse_total
        product = jnp.where(same, weights * dscores, 0.0)
        center = center + jnp.sum(product, axis=1, keepdims=True)
        rounded = weights.astype(jnp.bfloat16)
        spread = product.astype(jnp.bfloat16)
        output = output + jnp.dot(rounded, value_rows, preferred_element_type=jnp.float32)
        spread_sum = spread_sum + jnp.dot(spread, value_rows, preferred_element_type=jnp.float32)
        dvalue_sum = dvalue_sum + jnp.dot(rounded, dvalue_rows, preferred_element_type=jnp.float32)
        return center, output, spread_sum, dvalue_sum

    empty = jnp.zeros((BLOCK, HEAD_DIM), jnp.float32)
    center, output, spread_sum, dvalue_sum = lax.fori_loop(
        first, last, sums, (jnp.zeros((BLOCK, 1), jnp.float32), empty, empty, empty)
    )
    result_ref[0] = output.astype(result_ref.dtype)
    result_ref[1] = (spread_sum - center * output + dvalue_sum).astype(result_ref.dtype)


def attend(stacked, values, heads, offset, first_block, last_block, sample_ends, result_dtype):
    sources = stacked.shape[0]
    all_heads = values.shape[1] // 2

    def query_spec(t):
        return pl.BlockSpec((None, None, BLOCK, HEAD_DIM), lambda h, i, *_: (i, t * heads + h, 0, 0))

    def key_spec(t):
        return pl.BlockSpec((sources, None, BLOCK, HEAD_DIM), lambda h, i, *_: (0, t * heads + h, 0, 0))

    def value_spec(t):
        return pl.BlockSpec(
            (sources, None, BLOCK, HEAD_DIM), lambda h, i, *_: (0, t * all_heads + offset + h, 0, 0)
        )

    grid_spec = pltpu.PrefetchScalarGridSpec(
        num_scalar_prefetch=3,
        grid=(heads, sources),
        in_specs=[query_spec(0), query_spec(1), key_spec(2), key_spec(3), value_spec(0), value_spec(1)],
        out_specs=pl.BlockSpec((None, 2, BLOCK, HEAD_DIM), lambda h, i, *_: (i, 0, 0, h)),
    )
    return pl.pallas_call(
        attention_kernel,
        grid_spec=grid_spec,
        out_shape=jax.ShapeDtypeStruct((sources, 2, BLOCK, heads * HEAD_DIM), result_dtype),
        compiler_params=pltpu.CompilerParams(
            dimension_semantics=("arbitrary", "arbitrary"),
        ),
    )(first_block, last_block, sample_ends, stacked, stacked, stacked, stacked, values, values)


def gather_kernel(*refs):
    *sources, out_ref = refs
    per_step = out_ref.shape[0]
    heads = out_ref.shape[1] // len(sources)
    for d in range(per_step):
        for t, ref in enumerate(sources):
            for h in range(heads):
                column = (d * heads + h) * HEAD_DIM
                out_ref[d, t * heads + h] = ref[:, column:column + HEAD_DIM]


GATHER_STEPS = 2


def by_destination_all(arrays, destinations):
    tokens, width = arrays[0].shape[1], arrays[0].shape[2]
    local_width = width // destinations
    heads = local_width // HEAD_DIM
    steps = GATHER_STEPS if destinations % GATHER_STEPS == 0 else 1
    per_step = destinations // steps
    in_spec = pl.BlockSpec((None, tokens, per_step * local_width), lambda d: (0, 0, d))
    return pl.pallas_call(
        gather_kernel,
        grid=(steps,),
        in_specs=[in_spec] * len(arrays),
        out_specs=pl.BlockSpec(
            (per_step, len(arrays) * heads, tokens, HEAD_DIM), lambda d: (d, 0, 0, 0)
        ),
        out_shape=jax.ShapeDtypeStruct(
            (destinations, len(arrays) * heads, tokens, HEAD_DIM), arrays[0].dtype
        ),
    )(*arrays)


def assemble_kernel(offset, local_width, received_ref, *refs):
    out_ref, tan_ref, staged, widened, load_sem, store_sems = refs[-6:]
    sources, _, _, part_width = staged.shape
    load = pltpu.make_async_copy(received_ref, staged, load_sem)
    load.start()
    load.wait()
    stores = []
    for s in range(sources):
        column = s * local_width + offset
        for p, target in enumerate((out_ref, tan_ref)):
            widened[p, s] = staged[s, p].astype(jnp.float32)
            store = pltpu.make_async_copy(
                widened.at[p, s], target.at[0, :, pl.ds(column, part_width)], store_sems.at[p, s]
            )
            store.start()
            stores.append(store)
    for store in stores:
        store.wait()


def assemble_part(received, offset, previous, tokens, width):
    sources, _, _, part_width = received.shape
    operands = [received]
    aliases = {}
    if previous is not None:
        operands += list(previous)
        aliases = {1: 0, 2: 1}
    return pl.pallas_call(
        functools.partial(assemble_kernel, offset, width // sources),
        in_specs=[pl.BlockSpec(memory_space=pl.ANY)] * len(operands),
        out_specs=[pl.BlockSpec(memory_space=pl.ANY), pl.BlockSpec(memory_space=pl.ANY)],
        out_shape=[
            jax.ShapeDtypeStruct((1, tokens, width), jnp.float32),
            jax.ShapeDtypeStruct((1, tokens, width), jnp.float32),
        ],
        scratch_shapes=[
            pltpu.VMEM((sources, 2, tokens, part_width), received.dtype),
            pltpu.VMEM((2, sources, tokens, part_width), jnp.float32),
            pltpu.SemaphoreType.DMA(()),
            pltpu.SemaphoreType.DMA((2, sources)),
        ],
        input_output_aliases=aliases,
    )(*operands)


CHUNKS = 4
RESULT_DTYPE = jnp.bfloat16


def per_device_body(
    q_proj, q_tangent, k_proj, k_tangent, v_proj, v_tangent, query_norm_gain, key_norm_gain, lengths
):
    seq_count = lax.axis_size("seq")
    tokens = q_proj.shape[1]
    width = q_proj.shape[2]
    local_heads = width // HEAD_DIM // seq_count
    pack_tokens = tokens * seq_count
    chunks = min(CHUNKS, local_heads)
    chunk_heads = local_heads // chunks

    assert tokens == BLOCK

    def by_destination(array, heads):
        split = array.reshape(tokens, seq_count, local_heads, HEAD_DIM)[:, :, heads]
        return jnp.transpose(split, (1, 2, 0, 3))

    value_payload = by_destination_all((v_proj, v_tangent), seq_count)
    values = lax.all_to_all(value_payload, "seq", split_axis=0, concat_axis=0, tiled=True)

    q_normed, dq_normed = normalize(q_proj, q_tangent, query_norm_gain)
    k_normed, dk_normed = normalize(k_proj, k_tangent, key_norm_gain)
    own_row = lax.dynamic_slice_in_dim(lengths, lax.axis_index("samp"), 1, 0)[0]
    first_block, last_block, sample_ends = block_tables(own_row, pack_tokens)
    normed = (q_normed, dq_normed, k_normed, dk_normed)
    results = []
    for c in range(chunks):
        heads = slice(c * chunk_heads, (c + 1) * chunk_heads)
        payload = jnp.concatenate([by_destination(array, heads) for array in normed], axis=1)
        stacked = lax.all_to_all(payload, "seq", split_axis=0, concat_axis=0, tiled=True)
        result = attend(
            stacked, values, chunk_heads, c * chunk_heads,
            first_block, last_block, sample_ends, RESULT_DTYPE,
        )
        results.append(result)
    split = max(1, len(results) - 1)
    groups = [members for members in (results[:split], results[split:]) if members]
    outputs = None
    offset = 0
    for members in groups:
        group = jnp.concatenate(members, axis=3)
        received = lax.all_to_all(group, "seq", split_axis=0, concat_axis=0, tiled=True)
        outputs = assemble_part(received, offset, outputs, tokens, width)
        offset += group.shape[3]
    return tuple(outputs)


def solution(mesh):
    placed = (
        P(("groups", "samp"), "seq", None),
        P(("groups", "samp"), "seq", None),
        P(("groups", "samp"), "seq", None),
        P(("groups", "samp"), "seq", None),
        P(("groups", "samp"), "seq", None),
        P(("groups", "samp"), "seq", None),
        P(),
        P(),
        P("groups", None),
    )
    return jax.shard_map(
        per_device_body,
        mesh=mesh,
        in_specs=placed,
        out_specs=(P(("groups", "samp"), "seq", None), P(("groups", "samp"), "seq", None)),
        check_vma=False,
    )
```
